512 devices in a mesh: pipe: 16 (over x_lo, z), dp: 32 (over y, x_hi, core).
Axes of the slice: x: 4 (x_hi: 2, x_lo: 2; x = x_hi * 2 + x_lo), y: 8, z: 8, core: 2. Of those that a mesh axis runs over, the one named last changes fastest.
Arguments:
- section_input: bfloat16 [16, 4096, 4096], P('pipe', 'dp'), may hold values from -6 to 6
- out_grad: bfloat16 [16, 4096, 4096], P('pipe', 'dp'), may hold values from -6 to 6
- short_filter: bfloat16 [16, 2, 7, 4096], P('pipe', None, None, 'dp'), may hold values from -2 to 2
- long_filter: bfloat16 [16, 2, 256, 128], P('pipe', None, 'dp'), may hold values from -0.5 to 0.5
Outputs:
- passed_grad: bfloat16 [16, 4096, 4096], P('pipe', 'dp')
- short_grad: float32 [16, 2, 7, 4096], P('pipe', None, None, 'dp')
- long_grad: float32 [16, 2, 256, 128], P('pipe', None, 'dp')
The draws below stay inside these ranges and needn't reach their ends.
All inputs are finite; a program needn't handle non-finite values.
Results may differ from the reference program's by a relative error of at most 0.0058.
Values may be sent and summed in bfloat16 or wider, within the bound.
No kernel may reach another device: no remote copies, remote signals or barrier semaphores. Data moves between devices by JAX's collectives and lax.ppermute only.
A program may use at most 64 MiB of HBM per device.

```python
import jax
import jax.numpy as jnp
from jax import lax

C = 4096
K = 128
SHORT = 7
BLOCKS = 2
GROUPS = 256
SECTIONS = 16
SEQ = 4096


def levels(rng, dims, shards, low, largest):
    def one(dim, shards_of):
        heights = jax.random.uniform(jax.random.fold_in(jax.random.fold_in(rng, 6), dim), (shards_of,), jnp.float32, low / len(shards), largest / len(shards))
        return jnp.repeat(jnp.exp(heights), dims[dim] // shards_of).reshape((-1,) + (1,) * (len(dims) - dim - 1))

    gain = one(*shards[0])
    for cut in shards[1:]:
        gain = gain * one(*cut)
    return gain


def scatter_about(own_key, dims, scale, most, cuts=(), kind=jnp.bfloat16):
    values = jax.random.normal(own_key, dims, jnp.float32) * scale
    if len(cuts) > 0:
        values = levels(own_key, dims, cuts, -0.22, 0.18) * values
    return jnp.clip(values, min=-most, max=most).astype(kind)


def setup_inputs(seed: int = 0) -> dict:
    keys = jax.random.split(jax.random.key(seed), 5)
    return {
        "section_input": scatter_about(keys[0], (SECTIONS, SEQ, C), 1.0, 6.0, ((0, 16), (1, 32))),
        "out_grad": scatter_about(keys[1], (SECTIONS, SEQ, C), 1.0, 6.0, ((0, 16), (1, 32))),
        "short_filter": scatter_about(keys[2], (SECTIONS, BLOCKS, SHORT, C), SHORT ** -0.5, 2.0, ((0, 16), (3, 32))),
        "long_filter": scatter_about(keys[3], (SECTIONS, BLOCKS, GROUPS, K), K ** -0.5, 0.5, ((0, 16), (2, 32))),
    }


band_rows = 32


def band_tables(taps):
    band_count = taps // band_rows + 1
    first = jnp.arange(band_count, dtype=jnp.int32)[:, None, None] * band_rows
    row_pos = jnp.arange(band_rows, dtype=jnp.int32)[None, :, None]
    col_pos = jnp.arange(band_rows, dtype=jnp.int32)[None, None, :]
    lags = (first + row_pos - col_pos).reshape(-1)
    onehot = lags[:, None] == jnp.arange(taps, dtype=jnp.int32)[None, :]
    return onehot.astype(jnp.bfloat16).T, onehot.astype(jnp.float32)


def make_bands(filt, spread):
    groups = filt.shape[0]
    flat = jnp.dot(filt, spread, preferred_element_type=jnp.float32).astype(jnp.bfloat16)
    return flat.reshape(groups, -1, band_rows, band_rows).transpose(1, 0, 2, 3)


def as_blocks(field, groups):
    return field.reshape(-1, band_rows, groups, field.shape[1] // groups).astype(jnp.float32)


def causal_mix(padded, bands, block_count):
    band_count, groups = bands.shape[0], bands.shape[1]
    blocks = as_blocks(padded, groups)
    weights = bands.astype(jnp.float32)
    total = jnp.zeros((block_count, band_rows, groups, blocks.shape[3]), jnp.float32)
    for band in range(band_count):
        start = band_count - 1 - band
        total = total + jnp.einsum("gij,bjgc->bigc", weights[band], blocks[start:start + block_count])
    return total.reshape(block_count * band_rows, -1)


def anti_mix(padded, bands, block_count):
    band_count, groups = bands.shape[0], bands.shape[1]
    blocks = as_blocks(padded, groups)
    weights = bands.astype(jnp.float32)
    total = jnp.zeros((block_count, band_rows, groups, blocks.shape[3]), jnp.float32)
    for band in range(band_count):
        total = total + jnp.einsum("gij,bigc->bjgc", weights[band], blocks[band:band + block_count])
    return total.reshape(block_count * band_rows, -1)


def lag_past(grad, padded, collect, groups, band_count):
    grad_blocks = as_blocks(grad, groups)
    value_blocks = as_blocks(padded, groups)
    block_count = grad_blocks.shape[0]
    pieces = []
    for band in range(band_count):
        start = band_count - 1 - band
        pieces.append(jnp.einsum("bigc,bjgc->gij", grad_blocks, value_blocks[start:start + block_count]))
    stacked = jnp.stack(pieces, axis=1).reshape(groups, -1)
    return jnp.dot(stacked, collect, precision=lax.Precision.HIGHEST)


def short_mix(padded, taps_row, row_count):
    reach = taps_row.shape[0] - 1
    total = jnp.zeros((row_count, padded.shape[1]), jnp.float32)
    for tap_index in range(taps_row.shape[0]):
        start = reach - tap_index
        total = total + taps_row[tap_index].astype(jnp.float32) * padded[start:start + row_count].astype(jnp.float32)
    return total


def short_back(padded, taps_row, row_count):
    total = jnp.zeros((row_count, padded.shape[1]), jnp.float32)
    for tap_index in range(taps_row.shape[0]):
        total = total + taps_row[tap_index].astype(jnp.float32) * padded[tap_index:tap_index + row_count].astype(jnp.float32)
    return total


def short_corr(grad, padded, tap_count):
    reach = tap_count - 1
    row_count = grad.shape[0]
    grad_wide = grad.astype(jnp.float32)
    rows_out = []
    for tap_index in range(tap_count):
        start = reach - tap_index
        rows_out.append(jnp.sum(grad_wide * padded[start:start + row_count].astype(jnp.float32), axis=0))
    return jnp.stack(rows_out)


def section_backward(first_input, top_grad, short_all, long_all):
    seq_rows, width = first_input.shape
    groups, taps = long_all.shape[1], long_all.shape[2]
    tap_count = short_all.shape[1]
    reach = tap_count - 1
    band_count = taps // band_rows + 1
    spread, collect = band_tables(taps)
    block_count = seq_rows // band_rows
    first_bands = make_bands(long_all[0], spread)
    second_bands = make_bands(long_all[1], spread)
    tap_zeros = jnp.zeros((taps, width), jnp.bfloat16)
    reach_zeros = jnp.zeros((reach, width), jnp.bfloat16)
    input_past = jnp.concatenate([reach_zeros, first_input])
    mixed_one = short_mix(input_past, short_all[0], seq_rows).astype(jnp.bfloat16)
    mixed_one_past = jnp.concatenate([tap_zeros, mixed_one])
    long_one = causal_mix(mixed_one_past, first_bands, block_count)
    middle = (first_input.astype(jnp.float32) + long_one).astype(jnp.bfloat16)
    middle_past = jnp.concatenate([reach_zeros, middle])
    mixed_two = short_mix(middle_past, short_all[1], seq_rows).astype(jnp.bfloat16)
    grad_after = jnp.concatenate([top_grad, tap_zeros])
    dmix_two = anti_mix(grad_after, second_bands, block_count).astype(jnp.bfloat16)
    dlong_two = lag_past(top_grad, jnp.concatenate([tap_zeros, mixed_two]), collect, groups, band_count)
    back_two = short_back(jnp.concatenate([dmix_two, reach_zeros]), short_all[1], seq_rows)
    middle_grad = (top_grad.astype(jnp.float32) + back_two).astype(jnp.bfloat16)
    dshort_two = short_corr(dmix_two, middle_past, tap_count)
    middle_after = jnp.concatenate([middle_grad, tap_zeros])
    dmix_one = anti_mix(middle_after, first_bands, block_count).astype(jnp.bfloat16)
    dlong_one = lag_past(middle_grad, mixed_one_past, collect, groups, band_count)
    back_one = short_back(jnp.concatenate([dmix_one, reach_zeros]), short_all[0], seq_rows)
    input_grad = (middle_grad.astype(jnp.float32) + back_one).astype(jnp.bfloat16)
    dshort_one = short_corr(dmix_one, input_past, tap_count)
    return input_grad, jnp.stack([dshort_one, dshort_two]), jnp.stack([dlong_one, dlong_two])


def reference(section_input, out_grad, short_filter, long_filter):
    def one_section(index):
        return section_backward(section_input[index], out_grad[index], short_filter[index], long_filter[index])

    input_grad, short_grad, long_grad = lax.map(one_section, jnp.arange(SECTIONS, dtype=jnp.int32))
    passed_grad = jnp.concatenate([input_grad[1:], jnp.zeros_like(input_grad[:1])], axis=0)
    factor = float(SEQ) ** -0.5
    return passed_grad, short_grad * factor, long_grad * factor
```

```python
import jax
import jax.numpy as jnp
from jax import lax
from jax.sharding import PartitionSpec as P


def from_behind(shard, axis, by):
    devices = lax.axis_size(axis)
    pairs = [(i, i + by) for i in range(devices) if 0 <= i + by < devices]
    return lax.ppermute(shard, axis, pairs)


def circulants(long_pair):
    pair_count, group_count, taps = long_pair.shape
    row_pos = jnp.arange(taps, dtype=jnp.int32)[:, None]
    col_pos = jnp.arange(taps, dtype=jnp.int32)[None, :]
    lag_table = (col_pos - row_pos + taps) % taps
    table = (lag_table.reshape(1, -1) == jnp.arange(taps, dtype=jnp.int32)[:, None]).astype(
        jnp.bfloat16
    )
    flat = jnp.dot(long_pair.reshape(-1, taps), table, preferred_element_type=jnp.float32).astype(
        jnp.bfloat16
    )
    circ = flat.reshape(pair_count, group_count, taps, taps)
    upper = row_pos <= col_pos
    zero_value = jnp.zeros((), jnp.bfloat16)
    return (jnp.where(upper, circ, zero_value), jnp.where(upper, zero_value, circ))


def as_groups(field, group_count, taps):
    return field.reshape(group_count, field.shape[0] // group_count, field.shape[1] // taps, taps)


def causal_long(field, circ_now, circ_past):
    group_count, taps = (circ_now.shape[0], circ_now.shape[2])
    blocks = as_groups(field, group_count, taps)
    earlier_blocks = jnp.concatenate([jnp.zeros_like(blocks[:, :, :1]), blocks[:, :, :-1]], axis=2)
    total = jnp.einsum("gcbt,gts->gcbs", blocks, circ_now, preferred_element_type=jnp.float32)
    total = total + jnp.einsum(
        "gcbt,gts->gcbs", earlier_blocks, circ_past, preferred_element_type=jnp.float32
    )
    return total.reshape(field.shape)


def anti_long(grad, circ_now, circ_past):
    group_count, taps = (circ_now.shape[0], circ_now.shape[2])
    blocks = as_groups(grad, group_count, taps)
    later_blocks = jnp.concatenate([blocks[:, :, 1:], jnp.zeros_like(blocks[:, :, :1])], axis=2)
    total = jnp.einsum("gcbs,gts->gcbt", blocks, circ_now, preferred_element_type=jnp.float32)
    total = total + jnp.einsum(
        "gcbs,gts->gcbt", later_blocks, circ_past, preferred_element_type=jnp.float32
    )
    return total.reshape(grad.shape)


def lag_grad(values, grad, group_count, taps):
    value_blocks = as_groups(values, group_count, taps)
    grad_blocks = as_groups(grad, group_count, taps)
    earlier_blocks = jnp.concatenate(
        [jnp.zeros_like(value_blocks[:, :, :1]), value_blocks[:, :, :-1]], axis=2
    )
    pairs_now = jnp.einsum(
        "gcbt,gcbs->gts", value_blocks, grad_blocks, preferred_element_type=jnp.float32
    )
    pairs_past = jnp.einsum(
        "gcbt,gcbs->gts", earlier_blocks, grad_blocks, preferred_element_type=jnp.float32
    )
    row_pos = jnp.arange(taps, dtype=jnp.int32)[:, None]
    col_pos = jnp.arange(taps, dtype=jnp.int32)[None, :]
    joined = jnp.where(row_pos <= col_pos, pairs_now, pairs_past)
    doubled = jnp.concatenate([joined, joined], axis=2).reshape(group_count, 2 * taps * taps)
    padded = jnp.concatenate([doubled, jnp.zeros((group_count, taps), jnp.float32)], axis=1)
    skewed = padded.reshape(group_count, taps, 2 * taps + 1)[:, :, :taps]
    return jnp.sum(skewed, axis=1)


def short_mix(field, taps_row):
    tap_count = taps_row.shape[0]
    extra = tap_count - 1
    row_count = field.shape[1]
    padded = jnp.concatenate([jnp.zeros((field.shape[0], extra), field.dtype), field], axis=1)
    total = jnp.zeros(field.shape, jnp.float32)
    for tap_index in range(tap_count):
        start = extra - tap_index
        total = total + taps_row[tap_index].astype(jnp.float32)[:, None] * padded[
            :, start : start + row_count
        ].astype(jnp.float32)
    return total


def short_back(field, taps_row):
    tap_count = taps_row.shape[0]
    extra = tap_count - 1
    row_count = field.shape[1]
    padded = jnp.concatenate([field, jnp.zeros((field.shape[0], extra), field.dtype)], axis=1)
    total = jnp.zeros(field.shape, jnp.float32)
    for tap_index in range(tap_count):
        total = total + taps_row[tap_index].astype(jnp.float32)[:, None] * padded[
            :, tap_index : tap_index + row_count
        ].astype(jnp.float32)
    return total


def short_corr(grad, field, tap_count):
    extra = tap_count - 1
    row_count = field.shape[1]
    padded = jnp.concatenate([jnp.zeros((field.shape[0], extra), field.dtype), field], axis=1)
    grad_wide = grad.astype(jnp.float32)
    rows_out = []
    for tap_index in range(tap_count):
        start = extra - tap_index
        rows_out.append(
            jnp.sum(grad_wide * padded[:, start : start + row_count].astype(jnp.float32), axis=1)
        )
    return jnp.stack(rows_out)


CHUNKS = 2


def chunk_grads(source, top_grad, short_all, long_all):
    group_count, taps = (long_all.shape[1], long_all.shape[2])
    tap_count = short_all.shape[1]
    circ_now, circ_past = circulants(long_all)
    mixed_one = short_mix(source, short_all[0]).astype(jnp.bfloat16)
    long_one = causal_long(mixed_one, circ_now[0], circ_past[0])
    middle = (source.astype(jnp.float32) + long_one).astype(jnp.bfloat16)
    mixed_two = short_mix(middle, short_all[1]).astype(jnp.bfloat16)
    dmix_two = anti_long(top_grad, circ_now[1], circ_past[1]).astype(jnp.bfloat16)
    dlong_two = lag_grad(mixed_two, top_grad, group_count, taps)
    middle_grad = (top_grad.astype(jnp.float32) + short_back(dmix_two, short_all[1])).astype(
        jnp.bfloat16
    )
    dshort_two = short_corr(dmix_two, middle, tap_count)
    dmix_one = anti_long(middle_grad, circ_now[0], circ_past[0]).astype(jnp.bfloat16)
    dlong_one = lag_grad(mixed_one, middle_grad, group_count, taps)
    input_grad = (middle_grad.astype(jnp.float32) + short_back(dmix_one, short_all[0])).astype(
        jnp.bfloat16
    )
    dshort_one = short_corr(dmix_one, source, tap_count)
    return input_grad, jnp.stack([dshort_one, dshort_two]), jnp.stack([dlong_one, dlong_two])


def body(section_input, out_grad, short_filter, long_filter):
    devices = lax.axis_size("dp")
    rows, width = section_input.shape[1], section_input.shape[2]
    own = width // devices
    part = own // CHUNKS
    group_part = long_filter.shape[2] // CHUNKS
    both = jnp.stack([section_input[0], out_grad[0]]).reshape(2, rows, devices, own)
    passed, shorts, longs = [], [], []
    for index in range(CHUNKS):
        piece = both[:, :, :, index * part : (index + 1) * part].reshape(2, rows, devices * part)
        gathered = lax.all_to_all(piece, "dp", split_axis=2, concat_axis=1, tiled=True)
        source = gathered[0].T
        top_grad = gathered[1].T
        short_all = short_filter[0][:, :, index * part : (index + 1) * part]
        long_all = long_filter[0][:, index * group_part : (index + 1) * group_part]
        input_grad, short_grad, long_grad = chunk_grads(source, top_grad, short_all, long_all)
        own_rows = lax.all_to_all(input_grad.T, "dp", split_axis=0, concat_axis=1, tiled=True)
        passed.append(from_behind(own_rows.reshape(rows, devices, part), "pipe", -1))
        shorts.append(short_grad)
        longs.append(long_grad)
    passed_grad = jnp.concatenate(passed, axis=2).reshape(1, rows, width)
    factor = float(rows * devices) ** (-0.5)
    short_grad = jnp.concatenate(shorts, axis=2)[None] * factor
    long_grad = jnp.concatenate(longs, axis=1)[None] * factor
    return (passed_grad, short_grad, long_grad)


def solution(mesh):
    in_specs = (
        P("pipe", "dp", None),
        P("pipe", "dp", None),
        P("pipe", None, None, "dp"),
        P("pipe", None, "dp", None),
    )
    out_specs = (P("pipe", "dp", None), P("pipe", None, None, "dp"), P("pipe", None, "dp", None))
    return jax.shard_map(body, mesh=mesh, in_specs=in_specs, out_specs=out_specs, check_vma=False)
```

```python
import jax
import jax.numpy as jnp
from jax import lax
from jax.sharding import PartitionSpec as P


def from_behind(shard, axis, by):
    devices = lax.axis_size(axis)
    pairs = [(i, i + by) for i in range(devices) if 0 <= i + by < devices]
    return lax.ppermute(shard, axis, pairs)


def circulants(long_pair):
    pair_count, group_count, taps = long_pair.shape
    row_pos = jnp.arange(taps, dtype=jnp.int32)[:, None]
    col_pos = jnp.arange(taps, dtype=jnp.int32)[None, :]
    lag_table = (col_pos - row_pos + taps) % taps
    table = (lag_table.reshape(1, -1) == jnp.arange(taps, dtype=jnp.int32)[:, None]).astype(
        jnp.bfloat16
    )
    flat = jnp.dot(long_pair.reshape(-1, taps), table, preferred_element_type=jnp.float32).astype(
        jnp.bfloat16
    )
    circ = flat.reshape(pair_count, group_count, taps, taps)
    upper = row_pos <= col_pos
    zero_value = jnp.zeros((), jnp.bfloat16)
    return (jnp.where(upper, circ, zero_value), jnp.where(upper, zero_value, circ))


def as_groups(field, group_count, taps):
    return field.reshape(group_count, field.shape[0] // group_count, field.shape[1] // taps, taps)


def causal_long(field, circ_now, circ_past):
    group_count, taps = (circ_now.shape[0], circ_now.shape[2])
    blocks = as_groups(field, group_count, taps)
    earlier_blocks = jnp.concatenate([jnp.zeros_like(blocks[:, :, :1]), blocks[:, :, :-1]], axis=2)
    total = jnp.einsum("gcbt,gts->gcbs", blocks, circ_now, preferred_element_type=jnp.float32)
    total = total + jnp.einsum(
        "gcbt,gts->gcbs", earlier_blocks, circ_past, preferred_element_type=jnp.float32
    )
    return total.reshape(field.shape)


def anti_long(grad, circ_now, circ_past):
    group_count, taps = (circ_now.shape[0], circ_now.shape[2])
    blocks = as_groups(grad, group_count, taps)
    later_blocks = jnp.concatenate([blocks[:, :, 1:], jnp.zeros_like(blocks[:, :, :1])], axis=2)
    total = jnp.einsum("gcbs,gts->gcbt", blocks, circ_now, preferred_element_type=jnp.float32)
    total = total + jnp.einsum(
        "gcbs,gts->gcbt", later_blocks, circ_past, preferred_element_type=jnp.float32
    )
    return total.reshape(grad.shape)


def lag_grad(values, grad, group_count, taps):
    value_blocks = as_groups(values, group_count, taps)
    grad_blocks = as_groups(grad, group_count, taps)
    earlier_blocks = jnp.concatenate(
        [jnp.zeros_like(value_blocks[:, :, :1]), value_blocks[:, :, :-1]], axis=2
    )
    pairs_now = jnp.einsum(
        "gcbt,gcbs->gts", value_blocks, grad_blocks, preferred_element_type=jnp.float32
    )
    pairs_past = jnp.einsum(
        "gcbt,gcbs->gts", earlier_blocks, grad_blocks, preferred_element_type=jnp.float32
    )
    row_pos = jnp.arange(taps, dtype=jnp.int32)[:, None]
    col_pos = jnp.arange(taps, dtype=jnp.int32)[None, :]
    joined = jnp.where(row_pos <= col_pos, pairs_now, pairs_past)
    doubled = jnp.concatenate([joined, joined], axis=2).reshape(group_count, 2 * taps * taps)
    padded = jnp.concatenate([doubled, jnp.zeros((group_count, taps), jnp.float32)], axis=1)
    skewed = padded.reshape(group_count, taps, 2 * taps + 1)[:, :, :taps]
    return jnp.sum(skewed, axis=1)


def short_mix(field, taps_row):
    tap_count = taps_row.shape[0]
    extra = tap_count - 1
    row_count = field.shape[1]
    padded = jnp.concatenate([jnp.zeros((field.shape[0], extra), field.dtype), field], axis=1)
    total = jnp.zeros(field.shape, jnp.float32)
    for tap_index in range(tap_count):
        start = extra - tap_index
        total = total + taps_row[tap_index].astype(jnp.float32)[:, None] * padded[
            :, start : start + row_count
        ].astype(jnp.float32)
    return total


def short_back(field, taps_row):
    tap_count = taps_row.shape[0]
    extra = tap_count - 1
    row_count = field.shape[1]
    padded = jnp.concatenate([field, jnp.zeros((field.shape[0], extra), field.dtype)], axis=1)
    total = jnp.zeros(field.shape, jnp.float32)
    for tap_index in range(tap_count):
        total = total + taps_row[tap_index].astype(jnp.float32)[:, None] * padded[
            :, tap_index : tap_index + row_count
        ].astype(jnp.float32)
    return total


def short_corr(grad, field, tap_count):
    extra = tap_count - 1
    row_count = field.shape[1]
    padded = jnp.concatenate([jnp.zeros((field.shape[0], extra), field.dtype), field], axis=1)
    grad_wide = grad.astype(jnp.float32)
    rows_out = []
    for tap_index in range(tap_count):
        start = extra - tap_index
        rows_out.append(
            jnp.sum(grad_wide * padded[:, start : start + row_count].astype(jnp.float32), axis=1)
        )
    return jnp.stack(rows_out)


CHUNKS = 2


def chunk_grads(source, top_grad, short_all, long_all):
    group_count, taps = (long_all.shape[1], long_all.shape[2])
    tap_count = short_all.shape[1]
    circ_now, circ_past = circulants(long_all)
    mixed_one = short_mix(source, short_all[0]).astype(jnp.bfloat16)
    long_one = causal_long(mixed_one, circ_now[0], circ_past[0])
    middle = (source.astype(jnp.float32) + long_one).astype(jnp.bfloat16)
    mixed_two = short_mix(middle, short_all[1]).astype(jnp.bfloat16)
    dmix_two = anti_long(top_grad, circ_now[1], circ_past[1]).astype(jnp.bfloat16)
    dlong_two = lag_grad(mixed_two, top_grad, group_count, taps)
    middle_grad = (top_grad.astype(jnp.float32) + short_back(dmix_two, short_all[1])).astype(
        jnp.bfloat16
    )
    dshort_two = short_corr(dmix_two, middle, tap_count)
    dmix_one = anti_long(middle_grad, circ_now[0], circ_past[0]).astype(jnp.bfloat16)
    dlong_one = lag_grad(mixed_one, middle_grad, group_count, taps)
    input_grad = (middle_grad.astype(jnp.float32) + short_back(dmix_one, short_all[0])).astype(
        jnp.bfloat16
    )
    dshort_one = short_corr(dmix_one, source, tap_count)
    return input_grad, jnp.stack([dshort_one, dshort_two]), jnp.stack([dlong_one, dlong_two])


def body(section_input, out_grad, short_filter, long_filter):
    devices = lax.axis_size("dp")
    rows, width = section_input.shape[1], section_input.shape[2]
    both = jnp.stack([section_input[0], out_grad[0]])
    gathered = lax.all_to_all(both, "dp", split_axis=2, concat_axis=1, tiled=True)
    source = gathered[0].T
    top_grad = gathered[1].T
    input_grad, short_grad, long_grad = chunk_grads(source, top_grad, short_filter[0], long_filter[0])
    own = input_grad.shape[0]
    half = own // 2
    passed = []
    for index in range(2):
        piece = input_grad[index * half : (index + 1) * half].T
        own_rows = lax.all_to_all(piece, "dp", split_axis=0, concat_axis=1, tiled=True)
        passed.append(from_behind(own_rows.reshape(rows, devices, half), "pipe", -1))
    passed_grad = jnp.stack(passed, axis=2).reshape(1, rows, width)
    factor = float(rows * devices) ** (-0.5)
    return (passed_grad, short_grad[None] * factor, long_grad[None] * factor)


def solution(mesh):
    in_specs = (
        P("pipe", "dp", None),
        P("pipe", "dp", None),
        P("pipe", None, None, "dp"),
        P("pipe", None, "dp", None),
    )
    out_specs = (P("pipe", "dp", None), P("pipe", None, None, "dp"), P("pipe", None, "dp", None))
    return jax.shard_map(body, mesh=mesh, in_specs=in_specs, out_specs=out_specs, check_vma=False)
```

```python
import jax
import jax.numpy as jnp
from jax import lax
from jax.sharding import PartitionSpec as P


def from_behind(shard, axis, by):
    devices = lax.axis_size(axis)
    pairs = [(i, i + by) for i in range(devices) if 0 <= i + by < devices]
    return lax.ppermute(shard, axis, pairs)


def circulants(long_pair):
    pair_count, group_count, taps = long_pair.shape
    row_pos = jnp.arange(taps, dtype=jnp.int32)[:, None]
    col_pos = jnp.arange(taps, dtype=jnp.int32)[None, :]
    lag_table = (col_pos - row_pos + taps) % taps
    table = (lag_table.reshape(1, -1) == jnp.arange(taps, dtype=jnp.int32)[:, None]).astype(
        jnp.bfloat16
    )
    flat = jnp.dot(long_pair.reshape(-1, taps), table, preferred_element_type=jnp.float32).astype(
        jnp.bfloat16
    )
    circ = flat.reshape(pair_count, group_count, taps, taps)
    upper = row_pos <= col_pos
    zero_value = jnp.zeros((), jnp.bfloat16)
    return (jnp.where(upper, circ, zero_value), jnp.where(upper, zero_value, circ))


def as_groups(field, group_count, taps):
    return field.reshape(group_count, field.shape[0] // group_count, field.shape[1] // taps, taps)


def causal_long(field, circ_now, circ_past):
    group_count, taps = (circ_now.shape[0], circ_now.shape[2])
    blocks = as_groups(field, group_count, taps)
    earlier_blocks = jnp.concatenate([jnp.zeros_like(blocks[:, :, :1]), blocks[:, :, :-1]], axis=2)
    total = jnp.einsum("gcbt,gts->gcbs", blocks, circ_now, preferred_element_type=jnp.float32)
    total = total + jnp.einsum(
        "gcbt,gts->gcbs", earlier_blocks, circ_past, preferred_element_type=jnp.float32
    )
    return total.reshape(field.shape)


def anti_long(grad, circ_now, circ_past):
    group_count, taps = (circ_now.shape[0], circ_now.shape[2])
    blocks = as_groups(grad, group_count, taps)
    later_blocks = jnp.concatenate([blocks[:, :, 1:], jnp.zeros_like(blocks[:, :, :1])], axis=2)
    total = jnp.einsum("gcbs,gts->gcbt", blocks, circ_now, preferred_element_type=jnp.float32)
    total = total + jnp.einsum(
        "gcbs,gts->gcbt", later_blocks, circ_past, preferred_element_type=jnp.float32
    )
    return total.reshape(grad.shape)


def lag_grad(values, grad, group_count, taps):
    value_blocks = as_groups(values, group_count, taps)
    grad_blocks = as_groups(grad, group_count, taps)
    earlier_blocks = jnp.concatenate(
        [jnp.zeros_like(value_blocks[:, :, :1]), value_blocks[:, :, :-1]], axis=2
    )
    pairs_now = jnp.einsum(
        "gcbt,gcbs->gts", value_blocks, grad_blocks, preferred_element_type=jnp.float32
    )
    pairs_past = jnp.einsum(
        "gcbt,gcbs->gts", earlier_blocks, grad_blocks, preferred_element_type=jnp.float32
    )
    row_pos = jnp.arange(taps, dtype=jnp.int32)[:, None]
    col_pos = jnp.arange(taps, dtype=jnp.int32)[None, :]
    joined = jnp.where(row_pos <= col_pos, pairs_now, pairs_past)
    doubled = jnp.concatenate([joined, joined], axis=2).reshape(group_count, 2 * taps * taps)
    padded = jnp.concatenate([doubled, jnp.zeros((group_count, taps), jnp.float32)], axis=1)
    skewed = padded.reshape(group_count, taps, 2 * taps + 1)[:, :, :taps]
    return jnp.sum(skewed, axis=1)


def short_mix(field, taps_row):
    tap_count = taps_row.shape[0]
    extra = tap_count - 1
    row_count = field.shape[1]
    padded = jnp.concatenate([jnp.zeros((field.shape[0], extra), field.dtype), field], axis=1)
    total = jnp.zeros(field.shape, jnp.float32)
    for tap_index in range(tap_count):
        start = extra - tap_index
        total = total + taps_row[tap_index].astype(jnp.float32)[:, None] * padded[
            :, start : start + row_count
        ].astype(jnp.float32)
    return total


def short_back(field, taps_row):
    tap_count = taps_row.shape[0]
    extra = tap_count - 1
    row_count = field.shape[1]
    padded = jnp.concatenate([field, jnp.zeros((field.shape[0], extra), field.dtype)], axis=1)
    total = jnp.zeros(field.shape, jnp.float32)
    for tap_index in range(tap_count):
        total = total + taps_row[tap_index].astype(jnp.float32)[:, None] * padded[
            :, tap_index : tap_index + row_count
        ].astype(jnp.float32)
    return total


def short_corr(grad, field, tap_count):
    extra = tap_count - 1
    row_count = field.shape[1]
    padded = jnp.concatenate([jnp.zeros((field.shape[0], extra), field.dtype), field], axis=1)
    grad_wide = grad.astype(jnp.float32)
    rows_out = []
    for tap_index in range(tap_count):
        start = extra - tap_index
        rows_out.append(
            jnp.sum(grad_wide * padded[:, start : start + row_count].astype(jnp.float32), axis=1)
        )
    return jnp.stack(rows_out)


CHUNKS = 2


def chunk_grads(source, top_grad, short_all, long_all):
    group_count, taps = (long_all.shape[1], long_all.shape[2])
    tap_count = short_all.shape[1]
    circ_now, circ_past = circulants(long_all)
    mixed_one = short_mix(source, short_all[0]).astype(jnp.bfloat16)
    long_one = causal_long(mixed_one, circ_now[0], circ_past[0])
    middle = (source.astype(jnp.float32) + long_one).astype(jnp.bfloat16)
    mixed_two = short_mix(middle, short_all[1]).astype(jnp.bfloat16)
    dmix_two = anti_long(top_grad, circ_now[1], circ_past[1]).astype(jnp.bfloat16)
    dlong_two = lag_grad(mixed_two, top_grad, group_count, taps)
    middle_grad = (top_grad.astype(jnp.float32) + short_back(dmix_two, short_all[1])).astype(
        jnp.bfloat16
    )
    dshort_two = short_corr(dmix_two, middle, tap_count)
    dmix_one = anti_long(middle_grad, circ_now[0], circ_past[0]).astype(jnp.bfloat16)
    dlong_one = lag_grad(mixed_one, middle_grad, group_count, taps)
    input_grad = (middle_grad.astype(jnp.float32) + short_back(dmix_one, short_all[0])).astype(
        jnp.bfloat16
    )
    dshort_one = short_corr(dmix_one, source, tap_count)
    return input_grad, jnp.stack([dshort_one, dshort_two]), jnp.stack([dlong_one, dlong_two])


CHUNKS = 2


def body(section_input, out_grad, short_filter, long_filter):
    devices = lax.axis_size("dp")
    me = lax.axis_index("dp")
    rows, width = section_input.shape[1], section_input.shape[2]
    span = width // CHUNKS
    part = span // devices
    taps = long_filter.shape[3]
    group_width = width // (long_filter.shape[2] * devices)
    full_short = lax.all_gather(short_filter[0], "dp", axis=2, tiled=True)
    full_long = lax.all_gather(long_filter[0], "dp", axis=1, tiled=True)
    both = jnp.stack([section_input[0], out_grad[0]])
    passed, shorts, longs = [], [], []
    for index in range(CHUNKS):
        piece = both[:, :, index * span : (index + 1) * span]
        gathered = lax.all_to_all(piece, "dp", split_axis=2, concat_axis=1, tiled=True)
        first = index * span + me * part
        short_all = lax.dynamic_slice_in_dim(full_short, first, part, axis=2)
        long_all = lax.dynamic_slice_in_dim(full_long, first // group_width, part // group_width, axis=1)
        input_grad, short_grad, long_grad = chunk_grads(gathered[0].T, gathered[1].T, short_all, long_all)
        own_rows = lax.all_to_all(input_grad.T, "dp", split_axis=0, concat_axis=1, tiled=True)
        passed.append(from_behind(own_rows, "pipe", -1))
        shorts.append(short_grad)
        longs.append(long_grad)
    passed_grad = jnp.concatenate(passed, axis=1)[None]
    factor = float(rows * devices) ** (-0.5)
    every_short = lax.all_gather(jnp.stack(shorts), "dp", axis=0)
    every_short = every_short.transpose(2, 3, 1, 0, 4).reshape(2, -1, width)
    every_long = lax.all_gather(jnp.stack(longs), "dp", axis=0)
    every_long = every_long.transpose(2, 1, 0, 3, 4).reshape(2, -1, taps)
    own = width // devices
    own_groups = every_long.shape[1] // devices
    short_out = lax.dynamic_slice_in_dim(every_short, me * own, own, axis=2)
    long_out = lax.dynamic_slice_in_dim(every_long, me * own_groups, own_groups, axis=1)
    return (passed_grad, short_out[None] * factor, long_out[None] * factor)


def solution(mesh):
    in_specs = (
        P("pipe", "dp", None),
        P("pipe", "dp", None),
        P("pipe", None, None, "dp"),
        P("pipe", None, "dp", None),
    )
    out_specs = (P("pipe", "dp", None), P("pipe", None, None, "dp"), P("pipe", None, "dp", None))
    return jax.shard_map(body, mesh=mesh, in_specs=in_specs, out_specs=out_specs, check_vma=False)
```

```python
import jax
import jax.numpy as jnp
from jax import lax
from jax.sharding import PartitionSpec as P


def from_behind(shard, axis, by):
    devices = lax.axis_size(axis)
    pairs = [(i, i + by) for i in range(devices) if 0 <= i + by < devices]
    return lax.ppermute(shard, axis, pairs)


def circulants(long_pair):
    pair_count, group_count, taps = long_pair.shape
    row_pos = jnp.arange(taps, dtype=jnp.int32)[:, None]
    col_pos = jnp.arange(taps, dtype=jnp.int32)[None, :]
    lag_table = (col_pos - row_pos + taps) % taps
    table = (lag_table.reshape(1, -1) == jnp.arange(taps, dtype=jnp.int32)[:, None]).astype(
        jnp.bfloat16
    )
    flat = jnp.dot(long_pair.reshape(-1, taps), table, preferred_element_type=jnp.float32).astype(
        jnp.bfloat16
    )
    circ = flat.reshape(pair_count, group_count, taps, taps)
    upper = row_pos <= col_pos
    zero_value = jnp.zeros((), jnp.bfloat16)
    return (jnp.where(upper, circ, zero_value), jnp.where(upper, zero_value, circ))


def as_groups(field, group_count, taps):
    return field.reshape(group_count, field.shape[0] // group_count, field.shape[1] // taps, taps)


def causal_long(field, circ_now, circ_past):
    group_count, taps = (circ_now.shape[0], circ_now.shape[2])
    blocks = as_groups(field, group_count, taps)
    earlier_blocks = jnp.concatenate([jnp.zeros_like(blocks[:, :, :1]), blocks[:, :, :-1]], axis=2)
    total = jnp.einsum("gcbt,gts->gcbs", blocks, circ_now, preferred_element_type=jnp.float32)
    total = total + jnp.einsum(
        "gcbt,gts->gcbs", earlier_blocks, circ_past, preferred_element_type=jnp.float32
    )
    return total.reshape(field.shape)


def anti_long(grad, circ_now, circ_past):
    group_count, taps = (circ_now.shape[0], circ_now.shape[2])
    blocks = as_groups(grad, group_count, taps)
    later_blocks = jnp.concatenate([blocks[:, :, 1:], jnp.zeros_like(blocks[:, :, :1])], axis=2)
    total = jnp.einsum("gcbs,gts->gcbt", blocks, circ_now, preferred_element_type=jnp.float32)
    total = total + jnp.einsum(
        "gcbs,gts->gcbt", later_blocks, circ_past, preferred_element_type=jnp.float32
    )
    return total.reshape(grad.shape)


def lag_grad(values, grad, group_count, taps):
    value_blocks = as_groups(values, group_count, taps)
    grad_blocks = as_groups(grad, group_count, taps)
    earlier_blocks = jnp.concatenate(
        [jnp.zeros_like(value_blocks[:, :, :1]), value_blocks[:, :, :-1]], axis=2
    )
    pairs_now = jnp.einsum(
        "gcbt,gcbs->gts", value_blocks, grad_blocks, preferred_element_type=jnp.float32
    )
    pairs_past = jnp.einsum(
        "gcbt,gcbs->gts", earlier_blocks, grad_blocks, preferred_element_type=jnp.float32
    )
    row_pos = jnp.arange(taps, dtype=jnp.int32)[:, None]
    col_pos = jnp.arange(taps, dtype=jnp.int32)[None, :]
    joined = jnp.where(row_pos <= col_pos, pairs_now, pairs_past)
    doubled = jnp.concatenate([joined, joined], axis=2).reshape(group_count, 2 * taps * taps)
    padded = jnp.concatenate([doubled, jnp.zeros((group_count, taps), jnp.float32)], axis=1)
    skewed = padded.reshape(group_count, taps, 2 * taps + 1)[:, :, :taps]
    return jnp.sum(skewed, axis=1)


def short_mix(field, taps_row):
    tap_count = taps_row.shape[0]
    extra = tap_count - 1
    row_count = field.shape[1]
    padded = jnp.concatenate([jnp.zeros((field.shape[0], extra), field.dtype), field], axis=1)
    total = jnp.zeros(field.shape, jnp.float32)
    for tap_index in range(tap_count):
        start = extra - tap_index
        total = total + taps_row[tap_index].astype(jnp.float32)[:, None] * padded[
            :, start : start + row_count
        ].astype(jnp.float32)
    return total


def short_back(field, taps_row):
    tap_count = taps_row.shape[0]
    extra = tap_count - 1
    row_count = field.shape[1]
    padded = jnp.concatenate([field, jnp.zeros((field.shape[0], extra), field.dtype)], axis=1)
    total = jnp.zeros(field.shape, jnp.float32)
    for tap_index in range(tap_count):
        total = total + taps_row[tap_index].astype(jnp.float32)[:, None] * padded[
            :, tap_index : tap_index + row_count
        ].astype(jnp.float32)
    return total


def short_corr(grad, field, tap_count):
    extra = tap_count - 1
    row_count = field.shape[1]
    padded = jnp.concatenate([jnp.zeros((field.shape[0], extra), field.dtype), field], axis=1)
    grad_wide = grad.astype(jnp.float32)
    rows_out = []
    for tap_index in range(tap_count):
        start = extra - tap_index
        rows_out.append(
            jnp.sum(grad_wide * padded[:, start : start + row_count].astype(jnp.float32), axis=1)
        )
    return jnp.stack(rows_out)


CHUNKS = 2


def body(section_input, out_grad, short_filter, long_filter):
    devices = lax.axis_size("dp")
    rows, width = section_input.shape[1], section_input.shape[2]
    short_all = short_filter[0]
    long_all = long_filter[0]
    group_count, taps = (long_all.shape[1], long_all.shape[2])
    tap_count = short_all.shape[1]
    circ_now, circ_past = circulants(long_all)
    grad_rows = lax.all_to_all(out_grad[0], "dp", split_axis=1, concat_axis=0, tiled=True)
    grad_rows, later_input = lax.optimization_barrier((grad_rows, section_input[0]))
    input_rows = lax.all_to_all(later_input, "dp", split_axis=1, concat_axis=0, tiled=True)
    top_grad = grad_rows.T
    dmix_two = anti_long(top_grad, circ_now[1], circ_past[1]).astype(jnp.bfloat16)
    middle_grad = (top_grad.astype(jnp.float32) + short_back(dmix_two, short_all[1])).astype(
        jnp.bfloat16
    )
    dmix_one = anti_long(middle_grad, circ_now[0], circ_past[0]).astype(jnp.bfloat16)
    input_grad = (middle_grad.astype(jnp.float32) + short_back(dmix_one, short_all[0])).astype(
        jnp.bfloat16
    )
    own = input_grad.shape[0]
    half = own // 2
    passed = []
    for index in range(2):
        piece = input_grad[index * half : (index + 1) * half].T
        own_rows = lax.all_to_all(piece, "dp", split_axis=0, concat_axis=1, tiled=True)
        passed.append(from_behind(own_rows.reshape(rows, devices, half), "pipe", -1))
    passed_grad = jnp.stack(passed, axis=2).reshape(1, rows, width)
    source = input_rows.T
    mixed_one = short_mix(source, short_all[0]).astype(jnp.bfloat16)
    long_one = causal_long(mixed_one, circ_now[0], circ_past[0])
    middle = (source.astype(jnp.float32) + long_one).astype(jnp.bfloat16)
    mixed_two = short_mix(middle, short_all[1]).astype(jnp.bfloat16)
    dlong_two = lag_grad(mixed_two, top_grad, group_count, taps)
    dshort_two = short_corr(dmix_two, middle, tap_count)
    dlong_one = lag_grad(mixed_one, middle_grad, group_count, taps)
    dshort_one = short_corr(dmix_one, source, tap_count)
    factor = float(rows * devices) ** (-0.5)
    short_grad = jnp.stack([dshort_one, dshort_two])[None] * factor
    long_grad = jnp.stack([dlong_one, dlong_two])[None] * factor
    return (passed_grad, short_grad, long_grad)


def solution(mesh):
    in_specs = (
        P("pipe", "dp", None),
        P("pipe", "dp", None),
        P("pipe", None, None, "dp"),
        P("pipe", None, "dp", None),
    )
    out_specs = (P("pipe", "dp", None), P("pipe", None, None, "dp"), P("pipe", None, "dp", None))
    return jax.shard_map(body, mesh=mesh, in_specs=in_specs, out_specs=out_specs, check_vma=False)
```

```python
import jax
import jax.numpy as jnp
from jax import lax
from jax.sharding import PartitionSpec as P


def from_behind(shard, axis, by):
    devices = lax.axis_size(axis)
    pairs = [(i, i + by) for i in range(devices) if 0 <= i + by < devices]
    return lax.ppermute(shard, axis, pairs)


def circulants(long_pair):
    pair_count, group_count, taps = long_pair.shape
    row_pos = jnp.arange(taps, dtype=jnp.int32)[:, None]
    col_pos = jnp.arange(taps, dtype=jnp.int32)[None, :]
    lag_table = (col_pos - row_pos + taps) % taps
    table = (lag_table.reshape(1, -1) == jnp.arange(taps, dtype=jnp.int32)[:, None]).astype(
        jnp.bfloat16
    )
    flat = jnp.dot(long_pair.reshape(-1, taps), table, preferred_element_type=jnp.float32).astype(
        jnp.bfloat16
    )
    circ = flat.reshape(pair_count, group_count, taps, taps)
    upper = row_pos <= col_pos
    zero_value = jnp.zeros((), jnp.bfloat16)
    return (jnp.where(upper, circ, zero_value), jnp.where(upper, zero_value, circ))


def as_groups(field, group_count, taps):
    return field.reshape(group_count, field.shape[0] // group_count, field.shape[1] // taps, taps)


def causal_long(field, circ_now, circ_past):
    group_count, taps = (circ_now.shape[0], circ_now.shape[2])
    blocks = as_groups(field, group_count, taps)
    earlier_blocks = jnp.concatenate([jnp.zeros_like(blocks[:, :, :1]), blocks[:, :, :-1]], axis=2)
    total = jnp.einsum("gcbt,gts->gcbs", blocks, circ_now, preferred_element_type=jnp.float32)
    total = total + jnp.einsum(
        "gcbt,gts->gcbs", earlier_blocks, circ_past, preferred_element_type=jnp.float32
    )
    return total.reshape(field.shape)


def anti_long(grad, circ_now, circ_past):
    group_count, taps = (circ_now.shape[0], circ_now.shape[2])
    blocks = as_groups(grad, group_count, taps)
    later_blocks = jnp.concatenate([blocks[:, :, 1:], jnp.zeros_like(blocks[:, :, :1])], axis=2)
    total = jnp.einsum("gcbs,gts->gcbt", blocks, circ_now, preferred_element_type=jnp.float32)
    total = total + jnp.einsum(
        "gcbs,gts->gcbt", later_blocks, circ_past, preferred_element_type=jnp.float32
    )
    return total.reshape(grad.shape)


def lag_grad(values, grad, group_count, taps):
    value_blocks = as_groups(values, group_count, taps)
    grad_blocks = as_groups(grad, group_count, taps)
    earlier_blocks = jnp.concatenate(
        [jnp.zeros_like(value_blocks[:, :, :1]), value_blocks[:, :, :-1]], axis=2
    )
    pairs_now = jnp.einsum(
        "gcbt,gcbs->gts", value_blocks, grad_blocks, preferred_element_type=jnp.float32
    )
    pairs_past = jnp.einsum(
        "gcbt,gcbs->gts", earlier_blocks, grad_blocks, preferred_element_type=jnp.float32
    )
    row_pos = jnp.arange(taps, dtype=jnp.int32)[:, None]
    col_pos = jnp.arange(taps, dtype=jnp.int32)[None, :]
    joined = jnp.where(row_pos <= col_pos, pairs_now, pairs_past)
    doubled = jnp.concatenate([joined, joined], axis=2).reshape(group_count, 2 * taps * taps)
    padded = jnp.concatenate([doubled, jnp.zeros((group_count, taps), jnp.float32)], axis=1)
    skewed = padded.reshape(group_count, taps, 2 * taps + 1)[:, :, :taps]
    return jnp.sum(skewed, axis=1)


def short_mix(field, taps_row):
    tap_count = taps_row.shape[0]
    extra = tap_count - 1
    row_count = field.shape[1]
    padded = jnp.concatenate([jnp.zeros((field.shape[0], extra), field.dtype), field], axis=1)
    total = jnp.zeros(field.shape, jnp.float32)
    for tap_index in range(tap_count):
        start = extra - tap_index
        total = total + taps_row[tap_index].astype(jnp.float32)[:, None] * padded[
            :, start : start + row_count
        ].astype(jnp.float32)
    return total


def short_back(field, taps_row):
    tap_count = taps_row.shape[0]
    extra = tap_count - 1
    row_count = field.shape[1]
    padded = jnp.concatenate([field, jnp.zeros((field.shape[0], extra), field.dtype)], axis=1)
    total = jnp.zeros(field.shape, jnp.float32)
    for tap_index in range(tap_count):
        total = total + taps_row[tap_index].astype(jnp.float32)[:, None] * padded[
            :, tap_index : tap_index + row_count
        ].astype(jnp.float32)
    return total


def short_corr(grad, field, tap_count):
    extra = tap_count - 1
    row_count = field.shape[1]
    padded = jnp.concatenate([jnp.zeros((field.shape[0], extra), field.dtype), field], axis=1)
    grad_wide = grad.astype(jnp.float32)
    rows_out = []
    for tap_index in range(tap_count):
        start = extra - tap_index
        rows_out.append(
            jnp.sum(grad_wide * padded[:, start : start + row_count].astype(jnp.float32), axis=1)
        )
    return jnp.stack(rows_out)


CHUNKS = 2


def body(section_input, out_grad, short_filter, long_filter):
    devices = lax.axis_size("dp")
    rows, width = section_input.shape[1], section_input.shape[2]
    short_all = short_filter[0]
    long_all = long_filter[0]
    group_count, taps = (long_all.shape[1], long_all.shape[2])
    tap_count = short_all.shape[1]
    circ_now, circ_past = circulants(long_all)
    grad_rows = lax.all_to_all(out_grad[0], "dp", split_axis=1, concat_axis=0, tiled=True)
    grad_rows, later_input = lax.optimization_barrier((grad_rows, section_input[0]))
    input_rows = lax.all_to_all(later_input, "dp", split_axis=1, concat_axis=0, tiled=True)
    top_grad = grad_rows.T
    dmix_two = anti_long(top_grad, circ_now[1], circ_past[1]).astype(jnp.bfloat16)
    middle_grad = (top_grad.astype(jnp.float32) + short_back(dmix_two, short_all[1])).astype(
        jnp.bfloat16
    )
    dmix_one = anti_long(middle_grad, circ_now[0], circ_past[0]).astype(jnp.bfloat16)
    input_grad = (middle_grad.astype(jnp.float32) + short_back(dmix_one, short_all[0])).astype(
        jnp.bfloat16
    )
    input_rows, input_grad = lax.optimization_barrier((input_rows, input_grad))
    behind = from_behind(input_grad, "pipe", -1)
    own_rows = lax.all_to_all(behind.T, "dp", split_axis=0, concat_axis=1, tiled=True)
    passed_grad = own_rows[None]
    source = input_rows.T
    mixed_one = short_mix(source, short_all[0]).astype(jnp.bfloat16)
    long_one = causal_long(mixed_one, circ_now[0], circ_past[0])
    middle = (source.astype(jnp.float32) + long_one).astype(jnp.bfloat16)
    mixed_two = short_mix(middle, short_all[1]).astype(jnp.bfloat16)
    dlong_two = lag_grad(mixed_two, top_grad, group_count, taps)
    dshort_two = short_corr(dmix_two, middle, tap_count)
    dlong_one = lag_grad(mixed_one, middle_grad, group_count, taps)
    dshort_one = short_corr(dmix_one, source, tap_count)
    factor = float(rows * devices) ** (-0.5)
    short_grad = jnp.stack([dshort_one, dshort_two])[None] * factor
    long_grad = jnp.stack([dlong_one, dlong_two])[None] * factor
    return (passed_grad, short_grad, long_grad)


def solution(mesh):
    in_specs = (
        P("pipe", "dp", None),
        P("pipe", "dp", None),
        P("pipe", None, None, "dp"),
        P("pipe", None, "dp", None),
    )
    out_specs = (P("pipe", "dp", None), P("pipe", None, None, "dp"), P("pipe", None, "dp", None))
    return jax.shard_map(body, mesh=mesh, in_specs=in_specs, out_specs=out_specs, check_vma=False)
```

```python
import jax
import jax.numpy as jnp
from jax import lax
from jax.sharding import PartitionSpec as P


def from_behind(shard, axis, by):
    devices = lax.axis_size(axis)
    pairs = [(i, i + by) for i in range(devices) if 0 <= i + by < devices]
    return lax.ppermute(shard, axis, pairs)


def circulants(long_pair):
    pair_count, group_count, taps = long_pair.shape
    row_pos = jnp.arange(taps, dtype=jnp.int32)[:, None]
    col_pos = jnp.arange(taps, dtype=jnp.int32)[None, :]
    lag_table = (col_pos - row_pos + taps) % taps
    table = (lag_table.reshape(1, -1) == jnp.arange(taps, dtype=jnp.int32)[:, None]).astype(
        jnp.bfloat16
    )
    flat = jnp.dot(long_pair.reshape(-1, taps), table, preferred_element_type=jnp.float32).astype(
        jnp.bfloat16
    )
    circ = flat.reshape(pair_count, group_count, taps, taps)
    upper = row_pos <= col_pos
    zero_value = jnp.zeros((), jnp.bfloat16)
    return (jnp.where(upper, circ, zero_value), jnp.where(upper, zero_value, circ))


def as_groups(field, group_count, taps):
    return field.reshape(group_count, field.shape[0] // group_count, field.shape[1] // taps, taps)


def causal_long(field, circ_now, circ_past):
    group_count, taps = (circ_now.shape[0], circ_now.shape[2])
    blocks = as_groups(field, group_count, taps)
    earlier_blocks = jnp.concatenate([jnp.zeros_like(blocks[:, :, :1]), blocks[:, :, :-1]], axis=2)
    total = jnp.einsum("gcbt,gts->gcbs", blocks, circ_now, preferred_element_type=jnp.float32)
    total = total + jnp.einsum(
        "gcbt,gts->gcbs", earlier_blocks, circ_past, preferred_element_type=jnp.float32
    )
    return total.reshape(field.shape)


def anti_long(grad, circ_now, circ_past):
    group_count, taps = (circ_now.shape[0], circ_now.shape[2])
    blocks = as_groups(grad, group_count, taps)
    later_blocks = jnp.concatenate([blocks[:, :, 1:], jnp.zeros_like(blocks[:, :, :1])], axis=2)
    total = jnp.einsum("gcbs,gts->gcbt", blocks, circ_now, preferred_element_type=jnp.float32)
    total = total + jnp.einsum(
        "gcbs,gts->gcbt", later_blocks, circ_past, preferred_element_type=jnp.float32
    )
    return total.reshape(grad.shape)


def lag_grad(values, grad, group_count, taps):
    value_blocks = as_groups(values, group_count, taps)
    grad_blocks = as_groups(grad, group_count, taps)
    earlier_blocks = jnp.concatenate(
        [jnp.zeros_like(value_blocks[:, :, :1]), value_blocks[:, :, :-1]], axis=2
    )
    pairs_now = jnp.einsum(
        "gcbt,gcbs->gts", value_blocks, grad_blocks, preferred_element_type=jnp.float32
    )
    pairs_past = jnp.einsum(
        "gcbt,gcbs->gts", earlier_blocks, grad_blocks, preferred_element_type=jnp.float32
    )
    row_pos = jnp.arange(taps, dtype=jnp.int32)[:, None]
    col_pos = jnp.arange(taps, dtype=jnp.int32)[None, :]
    joined = jnp.where(row_pos <= col_pos, pairs_now, pairs_past)
    doubled = jnp.concatenate([joined, joined], axis=2).reshape(group_count, 2 * taps * taps)
    padded = jnp.concatenate([doubled, jnp.zeros((group_count, taps), jnp.float32)], axis=1)
    skewed = padded.reshape(group_count, taps, 2 * taps + 1)[:, :, :taps]
    return jnp.sum(skewed, axis=1)


def short_mix(field, taps_row):
    tap_count = taps_row.shape[0]
    extra = tap_count - 1
    row_count = field.shape[1]
    padded = jnp.concatenate([jnp.zeros((field.shape[0], extra), field.dtype), field], axis=1)
    total = jnp.zeros(field.shape, jnp.float32)
    for tap_index in range(tap_count):
        start = extra - tap_index
        total = total + taps_row[tap_index].astype(jnp.float32)[:, None] * padded[
            :, start : start + row_count
        ].astype(jnp.float32)
    return total


def short_back(field, taps_row):
    tap_count = taps_row.shape[0]
    extra = tap_count - 1
    row_count = field.shape[1]
    padded = jnp.concatenate([field, jnp.zeros((field.shape[0], extra), field.dtype)], axis=1)
    total = jnp.zeros(field.shape, jnp.float32)
    for tap_index in range(tap_count):
        total = total + taps_row[tap_index].astype(jnp.float32)[:, None] * padded[
            :, tap_index : tap_index + row_count
        ].astype(jnp.float32)
    return total


def short_corr(grad, field, tap_count):
    extra = tap_count - 1
    row_count = field.shape[1]
    padded = jnp.concatenate([jnp.zeros((field.shape[0], extra), field.dtype), field], axis=1)
    grad_wide = grad.astype(jnp.float32)
    rows_out = []
    for tap_index in range(tap_count):
        start = extra - tap_index
        rows_out.append(
            jnp.sum(grad_wide * padded[:, start : start + row_count].astype(jnp.float32), axis=1)
        )
    return jnp.stack(rows_out)


CHUNKS = 2


def body(section_input, out_grad, short_filter, long_filter):
    devices = lax.axis_size("dp")
    rows, width = section_input.shape[1], section_input.shape[2]
    short_all = short_filter[0]
    long_all = long_filter[0]
    group_count, taps = (long_all.shape[1], long_all.shape[2])
    tap_count = short_all.shape[1]
    circ_now, circ_past = circulants(long_all)
    grad_rows = lax.all_to_all(out_grad[0], "dp", split_axis=1, concat_axis=0, tiled=True)
    grad_rows, later_input = lax.optimization_barrier((grad_rows, section_input[0]))
    input_rows = lax.all_to_all(later_input, "dp", split_axis=1, concat_axis=0, tiled=True)
    top_grad = grad_rows.T
    own = top_grad.shape[0]
    half = own // 2
    group_half = group_count // 2
    dmix_twos, middle_grads, dmix_ones, behinds = [], [], [], []
    for index in range(2):
        rows_of = slice(index * half, (index + 1) * half)
        groups_of = slice(index * group_half, (index + 1) * group_half)
        grad_half = top_grad[rows_of]
        if index:
            grad_half, input_grad_h = lax.optimization_barrier((grad_half, input_grad_h))
            behinds.append(from_behind(input_grad_h, "pipe", -1))
        short_half = short_all[:, :, rows_of]
        dmix_two_h = anti_long(grad_half, circ_now[1, groups_of], circ_past[1, groups_of]).astype(jnp.bfloat16)
        middle_grad_h = (
            grad_half.astype(jnp.float32) + short_back(dmix_two_h, short_half[1])
        ).astype(jnp.bfloat16)
        dmix_one_h = anti_long(middle_grad_h, circ_now[0, groups_of], circ_past[0, groups_of]).astype(
            jnp.bfloat16
        )
        input_grad_h = (
            middle_grad_h.astype(jnp.float32) + short_back(dmix_one_h, short_half[0])
        ).astype(jnp.bfloat16)
        dmix_twos.append(dmix_two_h)
        middle_grads.append(middle_grad_h)
        dmix_ones.append(dmix_one_h)
    behinds.append(from_behind(input_grad_h, "pipe", -1))
    dmix_two = jnp.concatenate(dmix_twos)
    middle_grad = jnp.concatenate(middle_grads)
    dmix_one = jnp.concatenate(dmix_ones)
    input_rows, behind = lax.optimization_barrier((input_rows, jnp.concatenate(behinds)))
    own_rows = lax.all_to_all(behind.T, "dp", split_axis=0, concat_axis=1, tiled=True)
    passed_grad = own_rows[None]
    source = input_rows.T
    mixed_one = short_mix(source, short_all[0]).astype(jnp.bfloat16)
    long_one = causal_long(mixed_one, circ_now[0], circ_past[0])
    middle = (source.astype(jnp.float32) + long_one).astype(jnp.bfloat16)
    mixed_two = short_mix(middle, short_all[1]).astype(jnp.bfloat16)
    dlong_two = lag_grad(mixed_two, top_grad, group_count, taps)
    dshort_two = short_corr(dmix_two, middle, tap_count)
    dlong_one = lag_grad(mixed_one, middle_grad, group_count, taps)
    dshort_one = short_corr(dmix_one, source, tap_count)
    factor = float(rows * devices) ** (-0.5)
    short_grad = jnp.stack([dshort_one, dshort_two])[None] * factor
    long_grad = jnp.stack([dlong_one, dlong_two])[None] * factor
    return (passed_grad, short_grad, long_grad)


def solution(mesh):
    in_specs = (
        P("pipe", "dp", None),
        P("pipe", "dp", None),
        P("pipe", None, None, "dp"),
        P("pipe", None, "dp", None),
    )
    out_specs = (P("pipe", "dp", None), P("pipe", None, None, "dp"), P("pipe", None, "dp", None))
    return jax.shard_map(body, mesh=mesh, in_specs=in_specs, out_specs=out_specs, check_vma=False)
```

```python
import jax
import jax.numpy as jnp
from jax import lax
from jax.sharding import PartitionSpec as P


def from_behind(shard, axis, by):
    devices = lax.axis_size(axis)
    pairs = [(i, i + by) for i in range(devices) if 0 <= i + by < devices]
    return lax.ppermute(shard, axis, pairs)


def circulants(long_pair):
    pair_count, group_count, taps = long_pair.shape
    row_pos = jnp.arange(taps, dtype=jnp.int32)[:, None]
    col_pos = jnp.arange(taps, dtype=jnp.int32)[None, :]
    lag_table = (col_pos - row_pos + taps) % taps
    table = (lag_table.reshape(1, -1) == jnp.arange(taps, dtype=jnp.int32)[:, None]).astype(
        jnp.bfloat16
    )
    flat = jnp.dot(long_pair.reshape(-1, taps), table, preferred_element_type=jnp.float32).astype(
        jnp.bfloat16
    )
    circ = flat.reshape(pair_count, group_count, taps, taps)
    upper = row_pos <= col_pos
    zero_value = jnp.zeros((), jnp.bfloat16)
    return (jnp.where(upper, circ, zero_value), jnp.where(upper, zero_value, circ))


def as_groups(field, group_count, taps):
    return field.reshape(group_count, field.shape[0] // group_count, field.shape[1] // taps, taps)


def causal_long(field, circ_now, circ_past):
    group_count, taps = (circ_now.shape[0], circ_now.shape[2])
    blocks = as_groups(field, group_count, taps)
    earlier_blocks = jnp.concatenate([jnp.zeros_like(blocks[:, :, :1]), blocks[:, :, :-1]], axis=2)
    total = jnp.einsum("gcbt,gts->gcbs", blocks, circ_now, preferred_element_type=jnp.float32)
    total = total + jnp.einsum(
        "gcbt,gts->gcbs", earlier_blocks, circ_past, preferred_element_type=jnp.float32
    )
    return total.reshape(field.shape)


def anti_long(grad, circ_now, circ_past):
    group_count, taps = (circ_now.shape[0], circ_now.shape[2])
    blocks = as_groups(grad, group_count, taps)
    later_blocks = jnp.concatenate([blocks[:, :, 1:], jnp.zeros_like(blocks[:, :, :1])], axis=2)
    total = jnp.einsum("gcbs,gts->gcbt", blocks, circ_now, preferred_element_type=jnp.float32)
    total = total + jnp.einsum(
        "gcbs,gts->gcbt", later_blocks, circ_past, preferred_element_type=jnp.float32
    )
    return total.reshape(grad.shape)


def lag_grad(values, grad, group_count, taps):
    value_blocks = as_groups(values, group_count, taps)
    grad_blocks = as_groups(grad, group_count, taps)
    earlier_blocks = jnp.concatenate(
        [jnp.zeros_like(value_blocks[:, :, :1]), value_blocks[:, :, :-1]], axis=2
    )
    pairs_now = jnp.einsum(
        "gcbt,gcbs->gts", value_blocks, grad_blocks, preferred_element_type=jnp.float32
    )
    pairs_past = jnp.einsum(
        "gcbt,gcbs->gts", earlier_blocks, grad_blocks, preferred_element_type=jnp.float32
    )
    row_pos = jnp.arange(taps, dtype=jnp.int32)[:, None]
    col_pos = jnp.arange(taps, dtype=jnp.int32)[None, :]
    joined = jnp.where(row_pos <= col_pos, pairs_now, pairs_past)
    doubled = jnp.concatenate([joined, joined], axis=2).reshape(group_count, 2 * taps * taps)
    padded = jnp.concatenate([doubled, jnp.zeros((group_count, taps), jnp.float32)], axis=1)
    skewed = padded.reshape(group_count, taps, 2 * taps + 1)[:, :, :taps]
    return jnp.sum(skewed, axis=1)


def short_mix(field, taps_row):
    tap_count = taps_row.shape[0]
    extra = tap_count - 1
    row_count = field.shape[1]
    padded = jnp.concatenate([jnp.zeros((field.shape[0], extra), field.dtype), field], axis=1)
    total = jnp.zeros(field.shape, jnp.float32)
    for tap_index in range(tap_count):
        start = extra - tap_index
        total = total + taps_row[tap_index].astype(jnp.float32)[:, None] * padded[
            :, start : start + row_count
        ].astype(jnp.float32)
    return total


def short_back(field, taps_row):
    tap_count = taps_row.shape[0]
    extra = tap_count - 1
    row_count = field.shape[1]
    padded = jnp.concatenate([field, jnp.zeros((field.shape[0], extra), field.dtype)], axis=1)
    total = jnp.zeros(field.shape, jnp.float32)
    for tap_index in range(tap_count):
        total = total + taps_row[tap_index].astype(jnp.float32)[:, None] * padded[
            :, tap_index : tap_index + row_count
        ].astype(jnp.float32)
    return total


def short_corr(grad, field, tap_count):
    extra = tap_count - 1
    row_count = field.shape[1]
    padded = jnp.concatenate([jnp.zeros((field.shape[0], extra), field.dtype), field], axis=1)
    grad_wide = grad.astype(jnp.float32)
    rows_out = []
    for tap_index in range(tap_count):
        start = extra - tap_index
        rows_out.append(
            jnp.sum(grad_wide * padded[:, start : start + row_count].astype(jnp.float32), axis=1)
        )
    return jnp.stack(rows_out)


CHUNKS = 2


def body(section_input, out_grad, short_filter, long_filter):
    devices = lax.axis_size("dp")
    rows, width = section_input.shape[1], section_input.shape[2]
    short_all = short_filter[0]
    long_all = long_filter[0]
    group_count, taps = (long_all.shape[1], long_all.shape[2])
    tap_count = short_all.shape[1]
    circ_now, circ_past = circulants(long_all)
    grad_rows = lax.all_to_all(out_grad[0], "dp", split_axis=1, concat_axis=0, tiled=True)
    grad_rows, later_input = lax.optimization_barrier((grad_rows, section_input[0]))
    input_rows = lax.all_to_all(later_input, "dp", split_axis=1, concat_axis=0, tiled=True)
    top_grad = grad_rows.T
    own = top_grad.shape[0]
    half = own // 2
    group_half = group_count // 2
    dmix_twos, middle_grads, dmix_ones, behinds = [], [], [], []
    for index in range(2):
        rows_of = slice(index * half, (index + 1) * half)
        groups_of = slice(index * group_half, (index + 1) * group_half)
        grad_half = top_grad[rows_of]
        if index:
            grad_half, input_grad_h = lax.optimization_barrier((grad_half, input_grad_h))
            behinds.append(from_behind(input_grad_h, "pipe", -1))
        short_half = short_all[:, :, rows_of]
        dmix_two_h = anti_long(grad_half, circ_now[1, groups_of], circ_past[1, groups_of]).astype(jnp.bfloat16)
        middle_grad_h = (
            grad_half.astype(jnp.float32) + short_back(dmix_two_h, short_half[1])
        ).astype(jnp.bfloat16)
        dmix_one_h = anti_long(middle_grad_h, circ_now[0, groups_of], circ_past[0, groups_of]).astype(
            jnp.bfloat16
        )
        input_grad_h = (
            middle_grad_h.astype(jnp.float32) + short_back(dmix_one_h, short_half[0])
        ).astype(jnp.bfloat16)
        dmix_twos.append(dmix_two_h)
        middle_grads.append(middle_grad_h)
        dmix_ones.append(dmix_one_h)
    dmix_two = jnp.concatenate(dmix_twos)
    middle_grad = jnp.concatenate(middle_grads)
    dmix_one = jnp.concatenate(dmix_ones)
    input_rows, input_grad_h = lax.optimization_barrier((input_rows, input_grad_h))
    behinds.append(from_behind(input_grad_h, "pipe", -1))
    behind = jnp.concatenate(behinds)
    own_rows = lax.all_to_all(behind.T, "dp", split_axis=0, concat_axis=1, tiled=True)
    passed_grad = own_rows[None]
    source = input_rows.T
    mixed_one = short_mix(source, short_all[0]).astype(jnp.bfloat16)
    long_one = causal_long(mixed_one, circ_now[0], circ_past[0])
    middle = (source.astype(jnp.float32) + long_one).astype(jnp.bfloat16)
    mixed_two = short_mix(middle, short_all[1]).astype(jnp.bfloat16)
    dlong_two = lag_grad(mixed_two, top_grad, group_count, taps)
    dshort_two = short_corr(dmix_two, middle, tap_count)
    dlong_one = lag_grad(mixed_one, middle_grad, group_count, taps)
    dshort_one = short_corr(dmix_one, source, tap_count)
    factor = float(rows * devices) ** (-0.5)
    short_grad = jnp.stack([dshort_one, dshort_two])[None] * factor
    long_grad = jnp.stack([dlong_one, dlong_two])[None] * factor
    return (passed_grad, short_grad, long_grad)


def solution(mesh):
    in_specs = (
        P("pipe", "dp", None),
        P("pipe", "dp", None),
        P("pipe", None, None, "dp"),
        P("pipe", None, "dp", None),
    )
    out_specs = (P("pipe", "dp", None), P("pipe", None, None, "dp"), P("pipe", None, "dp", None))
    return jax.shard_map(body, mesh=mesh, in_specs=in_specs, out_specs=out_specs, check_vma=False)
```

```python
import jax
import jax.numpy as jnp
from jax import lax
from jax.sharding import PartitionSpec as P


def from_behind(shard, axis, by):
    devices = lax.axis_size(axis)
    pairs = [(i, i + by) for i in range(devices) if 0 <= i + by < devices]
    return lax.ppermute(shard, axis, pairs)


def circulants(long_pair):
    pair_count, group_count, taps = long_pair.shape
    row_pos = jnp.arange(taps, dtype=jnp.int32)[:, None]
    col_pos = jnp.arange(taps, dtype=jnp.int32)[None, :]
    lag_table = (col_pos - row_pos + taps) % taps
    table = (lag_table.reshape(1, -1) == jnp.arange(taps, dtype=jnp.int32)[:, None]).astype(
        jnp.bfloat16
    )
    flat = jnp.dot(long_pair.reshape(-1, taps), table, preferred_element_type=jnp.float32).astype(
        jnp.bfloat16
    )
    circ = flat.reshape(pair_count, group_count, taps, taps)
    upper = row_pos <= col_pos
    zero_value = jnp.zeros((), jnp.bfloat16)
    return (jnp.where(upper, circ, zero_value), jnp.where(upper, zero_value, circ))


def as_groups(field, group_count, taps):
    return field.reshape(group_count, field.shape[0] // group_count, field.shape[1] // taps, taps)


def causal_long(field, circ_now, circ_past):
    group_count, taps = (circ_now.shape[0], circ_now.shape[2])
    blocks = as_groups(field, group_count, taps)
    earlier_blocks = jnp.concatenate([jnp.zeros_like(blocks[:, :, :1]), blocks[:, :, :-1]], axis=2)
    total = jnp.einsum("gcbt,gts->gcbs", blocks, circ_now, preferred_element_type=jnp.float32)
    total = total + jnp.einsum(
        "gcbt,gts->gcbs", earlier_blocks, circ_past, preferred_element_type=jnp.float32
    )
    return total.reshape(field.shape)


def anti_long(grad, circ_now, circ_past):
    group_count, taps = (circ_now.shape[0], circ_now.shape[2])
    blocks = as_groups(grad, group_count, taps)
    later_blocks = jnp.concatenate([blocks[:, :, 1:], jnp.zeros_like(blocks[:, :, :1])], axis=2)
    total = jnp.einsum("gcbs,gts->gcbt", blocks, circ_now, preferred_element_type=jnp.float32)
    total = total + jnp.einsum(
        "gcbs,gts->gcbt", later_blocks, circ_past, preferred_element_type=jnp.float32
    )
    return total.reshape(grad.shape)


def lag_grad(values, grad, group_count, taps):
    value_blocks = as_groups(values, group_count, taps)
    grad_blocks = as_groups(grad, group_count, taps)
    earlier_blocks = jnp.concatenate(
        [jnp.zeros_like(value_blocks[:, :, :1]), value_blocks[:, :, :-1]], axis=2
    )
    pairs_now = jnp.einsum(
        "gcbt,gcbs->gts", value_blocks, grad_blocks, preferred_element_type=jnp.float32
    )
    pairs_past = jnp.einsum(
        "gcbt,gcbs->gts", earlier_blocks, grad_blocks, preferred_element_type=jnp.float32
    )
    row_pos = jnp.arange(taps, dtype=jnp.int32)[:, None]
    col_pos = jnp.arange(taps, dtype=jnp.int32)[None, :]
    joined = jnp.where(row_pos <= col_pos, pairs_now, pairs_past)
    doubled = jnp.concatenate([joined, joined], axis=2).reshape(group_count, 2 * taps * taps)
    padded = jnp.concatenate([doubled, jnp.zeros((group_count, taps), jnp.float32)], axis=1)
    skewed = padded.reshape(group_count, taps, 2 * taps + 1)[:, :, :taps]
    return jnp.sum(skewed, axis=1)


def short_mix(field, taps_row):
    tap_count = taps_row.shape[0]
    extra = tap_count - 1
    row_count = field.shape[1]
    padded = jnp.concatenate([jnp.zeros((field.shape[0], extra), field.dtype), field], axis=1)
    total = jnp.zeros(field.shape, jnp.float32)
    for tap_index in range(tap_count):
        start = extra - tap_index
        total = total + taps_row[tap_index].astype(jnp.float32)[:, None] * padded[
            :, start : start + row_count
        ].astype(jnp.float32)
    return total


def short_back(field, taps_row):
    tap_count = taps_row.shape[0]
    extra = tap_count - 1
    row_count = field.shape[1]
    padded = jnp.concatenate([field, jnp.zeros((field.shape[0], extra), field.dtype)], axis=1)
    total = jnp.zeros(field.shape, jnp.float32)
    for tap_index in range(tap_count):
        total = total + taps_row[tap_index].astype(jnp.float32)[:, None] * padded[
            :, tap_index : tap_index + row_count
        ].astype(jnp.float32)
    return total


def short_corr(grad, field, tap_count):
    extra = tap_count - 1
    row_count = field.shape[1]
    padded = jnp.concatenate([jnp.zeros((field.shape[0], extra), field.dtype), field], axis=1)
    grad_wide = grad.astype(jnp.float32)
    rows_out = []
    for tap_index in range(tap_count):
        start = extra - tap_index
        rows_out.append(
            jnp.sum(grad_wide * padded[:, start : start + row_count].astype(jnp.float32), axis=1)
        )
    return jnp.stack(rows_out)


CHUNKS = 2


def short_corr_rows(grad, field, tap_count):
    extra = tap_count - 1
    row_count = field.shape[0]
    padded = jnp.concatenate([jnp.zeros((extra, field.shape[1]), field.dtype), field], axis=0)
    grad_wide = grad.astype(jnp.float32)
    rows_out = []
    for tap_index in range(tap_count):
        start = extra - tap_index
        rows_out.append(
            jnp.sum(grad_wide * padded[start : start + row_count].astype(jnp.float32), axis=0)
        )
    return jnp.stack(rows_out)


def body(section_input, out_grad, short_filter, long_filter):
    devices = lax.axis_size("dp")
    rows, width = section_input.shape[1], section_input.shape[2]
    short_all = short_filter[0]
    long_all = long_filter[0]
    group_count, taps = (long_all.shape[1], long_all.shape[2])
    tap_count = short_all.shape[1]
    circ_now, circ_past = circulants(long_all)
    grad_rows = lax.all_to_all(out_grad[0], "dp", split_axis=1, concat_axis=0, tiled=True)
    grad_rows, later_input = lax.optimization_barrier((grad_rows, section_input[0]))
    input_rows = lax.all_to_all(later_input, "dp", split_axis=1, concat_axis=0, tiled=True)
    top_grad = grad_rows.T
    own = top_grad.shape[0]
    half = own // 2
    group_half = group_count // 2
    dmix_twos, middle_grads, dmix_ones, behinds = [], [], [], []
    for index in range(2):
        rows_of = slice(index * half, (index + 1) * half)
        groups_of = slice(index * group_half, (index + 1) * group_half)
        grad_half = top_grad[rows_of]
        if index:
            grad_half, input_grad_h = lax.optimization_barrier((grad_half, input_grad_h))
            behinds.append(from_behind(input_grad_h, "pipe", -1))
        short_half = short_all[:, :, rows_of]
        dmix_two_h = anti_long(grad_half, circ_now[1, groups_of], circ_past[1, groups_of]).astype(jnp.bfloat16)
        middle_grad_h = (
            grad_half.astype(jnp.float32) + short_back(dmix_two_h, short_half[1])
        ).astype(jnp.bfloat16)
        dmix_one_h = anti_long(middle_grad_h, circ_now[0, groups_of], circ_past[0, groups_of]).astype(
            jnp.bfloat16
        )
        input_grad_h = (
            middle_grad_h.astype(jnp.float32) + short_back(dmix_one_h, short_half[0])
        ).astype(jnp.bfloat16)
        dmix_twos.append(dmix_two_h)
        middle_grads.append(middle_grad_h)
        dmix_ones.append(dmix_one_h)
    dmix_two = jnp.concatenate(dmix_twos)
    middle_grad = jnp.concatenate(middle_grads)
    dmix_one = jnp.concatenate(dmix_ones)
    input_rows, input_grad_h = lax.optimization_barrier((input_rows, input_grad_h))
    behinds.append(from_behind(input_grad_h, "pipe", -1))
    behind = jnp.concatenate(behinds)
    own_rows = lax.all_to_all(behind.T, "dp", split_axis=0, concat_axis=1, tiled=True)
    passed_grad = own_rows[None]
    source = input_rows.T
    mixed_one = short_mix(source, short_all[0]).astype(jnp.bfloat16)
    long_one = causal_long(mixed_one, circ_now[0], circ_past[0])
    middle = (source.astype(jnp.float32) + long_one).astype(jnp.bfloat16)
    mixed_two = short_mix(middle, short_all[1]).astype(jnp.bfloat16)
    dlong_two = lag_grad(mixed_two, top_grad, group_count, taps)
    dshort_two = short_corr_rows(dmix_two.T, middle.T, tap_count)
    dlong_one = lag_grad(mixed_one, middle_grad, group_count, taps)
    dshort_one = short_corr_rows(dmix_one.T, input_rows, tap_count)
    factor = float(rows * devices) ** (-0.5)
    short_grad = jnp.stack([dshort_one, dshort_two])[None] * factor
    long_grad = jnp.stack([dlong_one, dlong_two])[None] * factor
    return (passed_grad, short_grad, long_grad)


def solution(mesh):
    in_specs = (
        P("pipe", "dp", None),
        P("pipe", "dp", None),
        P("pipe", None, None, "dp"),
        P("pipe", None, "dp", None),
    )
    out_specs = (P("pipe", "dp", None), P("pipe", None, None, "dp"), P("pipe", None, "dp", None))
    return jax.shard_map(body, mesh=mesh, in_specs=in_specs, out_specs=out_specs, check_vma=False)
```

```python
import jax
import jax.numpy as jnp
from jax import lax
from jax.sharding import PartitionSpec as P


def from_behind(shard, axis, by):
    devices = lax.axis_size(axis)
    pairs = [(i, i + by) for i in range(devices) if 0 <= i + by < devices]
    return lax.ppermute(shard, axis, pairs)


def circulants(long_pair):
    pair_count, group_count, taps = long_pair.shape
    row_pos = jnp.arange(taps, dtype=jnp.int32)[:, None]
    col_pos = jnp.arange(taps, dtype=jnp.int32)[None, :]
    lag_table = (col_pos - row_pos + taps) % taps
    table = (lag_table.reshape(1, -1) == jnp.arange(taps, dtype=jnp.int32)[:, None]).astype(
        jnp.bfloat16
    )
    flat = jnp.dot(long_pair.reshape(-1, taps), table, preferred_element_type=jnp.float32).astype(
        jnp.bfloat16
    )
    circ = flat.reshape(pair_count, group_count, taps, taps)
    upper = row_pos <= col_pos
    zero_value = jnp.zeros((), jnp.bfloat16)
    return (jnp.where(upper, circ, zero_value), jnp.where(upper, zero_value, circ))


def as_groups(field, group_count, taps):
    return field.reshape(group_count, field.shape[0] // group_count, field.shape[1] // taps, taps)


def causal_long(field, circ_now, circ_past):
    group_count, taps = (circ_now.shape[0], circ_now.shape[2])
    blocks = as_groups(field, group_count, taps)
    earlier_blocks = jnp.concatenate([jnp.zeros_like(blocks[:, :, :1]), blocks[:, :, :-1]], axis=2)
    total = jnp.einsum("gcbt,gts->gcbs", blocks, circ_now, preferred_element_type=jnp.float32)
    total = total + jnp.einsum(
        "gcbt,gts->gcbs", earlier_blocks, circ_past, preferred_element_type=jnp.float32
    )
    return total.reshape(field.shape)


def anti_long(grad, circ_now, circ_past):
    group_count, taps = (circ_now.shape[0], circ_now.shape[2])
    blocks = as_groups(grad, group_count, taps)
    later_blocks = jnp.concatenate([blocks[:, :, 1:], jnp.zeros_like(blocks[:, :, :1])], axis=2)
    total = jnp.einsum("gcbs,gts->gcbt", blocks, circ_now, preferred_element_type=jnp.float32)
    total = total + jnp.einsum(
        "gcbs,gts->gcbt", later_blocks, circ_past, preferred_element_type=jnp.float32
    )
    return total.reshape(grad.shape)


def lag_grad(values, grad, group_count, taps):
    value_blocks = as_groups(values, group_count, taps)
    grad_blocks = as_groups(grad, group_count, taps)
    earlier_blocks = jnp.concatenate(
        [jnp.zeros_like(value_blocks[:, :, :1]), value_blocks[:, :, :-1]], axis=2
    )
    pairs_now = jnp.einsum(
        "gcbt,gcbs->gts", value_blocks, grad_blocks, preferred_element_type=jnp.float32
    )
    pairs_past = jnp.einsum(
        "gcbt,gcbs->gts", earlier_blocks, grad_blocks, preferred_element_type=jnp.float32
    )
    row_pos = jnp.arange(taps, dtype=jnp.int32)[:, None]
    col_pos = jnp.arange(taps, dtype=jnp.int32)[None, :]
    joined = jnp.where(row_pos <= col_pos, pairs_now, pairs_past)
    doubled = jnp.concatenate([joined, joined], axis=2).reshape(group_count, 2 * taps * taps)
    padded = jnp.concatenate([doubled, jnp.zeros((group_count, taps), jnp.float32)], axis=1)
    skewed = padded.reshape(group_count, taps, 2 * taps + 1)[:, :, :taps]
    return jnp.sum(skewed, axis=1)


def short_mix(field, taps_row):
    tap_count = taps_row.shape[0]
    extra = tap_count - 1
    row_count = field.shape[1]
    padded = jnp.concatenate([jnp.zeros((field.shape[0], extra), field.dtype), field], axis=1)
    total = jnp.zeros(field.shape, jnp.float32)
    for tap_index in range(tap_count):
        start = extra - tap_index
        total = total + taps_row[tap_index].astype(jnp.float32)[:, None] * padded[
            :, start : start + row_count
        ].astype(jnp.float32)
    return total


def short_back(field, taps_row):
    tap_count = taps_row.shape[0]
    extra = tap_count - 1
    row_count = field.shape[1]
    padded = jnp.concatenate([field, jnp.zeros((field.shape[0], extra), field.dtype)], axis=1)
    total = jnp.zeros(field.shape, jnp.float32)
    for tap_index in range(tap_count):
        total = total + taps_row[tap_index].astype(jnp.float32)[:, None] * padded[
            :, tap_index : tap_index + row_count
        ].astype(jnp.float32)
    return total


def short_corr(grad, field, tap_count):
    extra = tap_count - 1
    row_count = field.shape[1]
    padded = jnp.concatenate([jnp.zeros((field.shape[0], extra), field.dtype), field], axis=1)
    grad_wide = grad.astype(jnp.float32)
    rows_out = []
    for tap_index in range(tap_count):
        start = extra - tap_index
        rows_out.append(
            jnp.sum(grad_wide * padded[:, start : start + row_count].astype(jnp.float32), axis=1)
        )
    return jnp.stack(rows_out)


CHUNKS = 2


def short_corr_rows(grad, field, tap_count):
    extra = tap_count - 1
    row_count = field.shape[0]
    padded = jnp.concatenate([jnp.zeros((extra, field.shape[1]), field.dtype), field], axis=0)
    grad_wide = grad.astype(jnp.float32)
    rows_out = []
    for tap_index in range(tap_count):
        start = extra - tap_index
        rows_out.append(
            jnp.sum(grad_wide * padded[start : start + row_count].astype(jnp.float32), axis=0)
        )
    return jnp.stack(rows_out)


def body(section_input, out_grad, short_filter, long_filter):
    devices = lax.axis_size("dp")
    rows, width = section_input.shape[1], section_input.shape[2]
    short_all = short_filter[0]
    long_all = long_filter[0]
    group_count, taps = (long_all.shape[1], long_all.shape[2])
    tap_count = short_all.shape[1]
    circ_now, circ_past = circulants(long_all)
    grad_rows = lax.all_to_all(out_grad[0], "dp", split_axis=1, concat_axis=0, tiled=True)
    grad_rows, later_input = lax.optimization_barrier((grad_rows, section_input[0]))
    input_rows = lax.all_to_all(later_input, "dp", split_axis=1, concat_axis=0, tiled=True)
    top_grad = grad_rows.T
    own = top_grad.shape[0]
    half = own // 2
    group_half = group_count // 2
    dmix_twos, middle_grads, dmix_ones, behinds = [], [], [], []
    for index in range(2):
        rows_of = slice(index * half, (index + 1) * half)
        groups_of = slice(index * group_half, (index + 1) * group_half)
        grad_half = top_grad[rows_of]
        if index:
            grad_half, input_grad_h = lax.optimization_barrier((grad_half, input_grad_h))
            behinds.append(from_behind(input_grad_h, "pipe", -1))
        short_half = short_all[:, :, rows_of]
        dmix_two_h = anti_long(grad_half, circ_now[1, groups_of], circ_past[1, groups_of]).astype(jnp.bfloat16)
        middle_grad_h = (
            grad_half.astype(jnp.float32) + short_back(dmix_two_h, short_half[1])
        ).astype(jnp.bfloat16)
        dmix_one_h = anti_long(middle_grad_h, circ_now[0, groups_of], circ_past[0, groups_of]).astype(
            jnp.bfloat16
        )
        input_grad_h = (
            middle_grad_h.astype(jnp.float32) + short_back(dmix_one_h, short_half[0])
        ).astype(jnp.bfloat16)
        dmix_twos.append(dmix_two_h)
        middle_grads.append(middle_grad_h)
        dmix_ones.append(dmix_one_h)
    dmix_two = jnp.concatenate(dmix_twos)
    middle_grad = jnp.concatenate(middle_grads)
    dmix_one = jnp.concatenate(dmix_ones)
    behinds.append(from_behind(input_grad_h, "pipe", -1))
    input_rows, _ = lax.optimization_barrier((input_rows, input_grad_h))
    behind = jnp.concatenate(behinds)
    own_rows = lax.all_to_all(behind.T, "dp", split_axis=0, concat_axis=1, tiled=True)
    passed_grad = own_rows[None]
    source = input_rows.T
    mixed_one = short_mix(source, short_all[0]).astype(jnp.bfloat16)
    long_one = causal_long(mixed_one, circ_now[0], circ_past[0])
    middle = (source.astype(jnp.float32) + long_one).astype(jnp.bfloat16)
    mixed_two = short_mix(middle, short_all[1]).astype(jnp.bfloat16)
    dlong_two = lag_grad(mixed_two, top_grad, group_count, taps)
    dshort_two = short_corr_rows(dmix_two.T, middle.T, tap_count)
    dlong_one = lag_grad(mixed_one, middle_grad, group_count, taps)
    dshort_one = short_corr_rows(dmix_one.T, input_rows, tap_count)
    factor = float(rows * devices) ** (-0.5)
    short_grad = jnp.stack([dshort_one, dshort_two])[None] * factor
    long_grad = jnp.stack([dlong_one, dlong_two])[None] * factor
    return (passed_grad, short_grad, long_grad)


def solution(mesh):
    in_specs = (
        P("pipe", "dp", None),
        P("pipe", "dp", None),
        P("pipe", None, None, "dp"),
        P("pipe", None, "dp", None),
    )
    out_specs = (P("pipe", "dp", None), P("pipe", None, None, "dp"), P("pipe", None, "dp", None))
    return jax.shard_map(body, mesh=mesh, in_specs=in_specs, out_specs=out_specs, check_vma=False)
```

```python
import jax
import jax.numpy as jnp
from jax import lax
from jax.sharding import PartitionSpec as P


def from_behind(shard, axis, by):
    devices = lax.axis_size(axis)
    pairs = [(i, i + by) for i in range(devices) if 0 <= i + by < devices]
    return lax.ppermute(shard, axis, pairs)


def circulants(long_pair):
    pair_count, group_count, taps = long_pair.shape
    row_pos = jnp.arange(taps, dtype=jnp.int32)[:, None]
    col_pos = jnp.arange(taps, dtype=jnp.int32)[None, :]
    lag_table = (col_pos - row_pos + taps) % taps
    table = (lag_table.reshape(1, -1) == jnp.arange(taps, dtype=jnp.int32)[:, None]).astype(
        jnp.bfloat16
    )
    flat = jnp.dot(long_pair.reshape(-1, taps), table, preferred_element_type=jnp.float32).astype(
        jnp.bfloat16
    )
    circ = flat.reshape(pair_count, group_count, taps, taps)
    upper = row_pos <= col_pos
    zero_value = jnp.zeros((), jnp.bfloat16)
    return (jnp.where(upper, circ, zero_value), jnp.where(upper, zero_value, circ))


def as_groups(field, group_count, taps):
    return field.reshape(group_count, field.shape[0] // group_count, field.shape[1] // taps, taps)


def causal_long(field, circ_now, circ_past):
    group_count, taps = (circ_now.shape[0], circ_now.shape[2])
    blocks = as_groups(field, group_count, taps)
    earlier_blocks = jnp.concatenate([jnp.zeros_like(blocks[:, :, :1]), blocks[:, :, :-1]], axis=2)
    total = jnp.einsum("gcbt,gts->gcbs", blocks, circ_now, preferred_element_type=jnp.float32)
    total = total + jnp.einsum(
        "gcbt,gts->gcbs", earlier_blocks, circ_past, preferred_element_type=jnp.float32
    )
    return total.reshape(field.shape)


def anti_long(grad, circ_now, circ_past):
    group_count, taps = (circ_now.shape[0], circ_now.shape[2])
    blocks = as_groups(grad, group_count, taps)
    later_blocks = jnp.concatenate([blocks[:, :, 1:], jnp.zeros_like(blocks[:, :, :1])], axis=2)
    total = jnp.einsum("gcbs,gts->gcbt", blocks, circ_now, preferred_element_type=jnp.float32)
    total = total + jnp.einsum(
        "gcbs,gts->gcbt", later_blocks, circ_past, preferred_element_type=jnp.float32
    )
    return total.reshape(grad.shape)


def lag_grad(values, grad, group_count, taps):
    value_blocks = as_groups(values, group_count, taps)
    grad_blocks = as_groups(grad, group_count, taps)
    earlier_blocks = jnp.concatenate(
        [jnp.zeros_like(value_blocks[:, :, :1]), value_blocks[:, :, :-1]], axis=2
    )
    pairs_now = jnp.einsum(
        "gcbt,gcbs->gts", value_blocks, grad_blocks, preferred_element_type=jnp.float32
    )
    pairs_past = jnp.einsum(
        "gcbt,gcbs->gts", earlier_blocks, grad_blocks, preferred_element_type=jnp.float32
    )
    row_pos = jnp.arange(taps, dtype=jnp.int32)[:, None]
    col_pos = jnp.arange(taps, dtype=jnp.int32)[None, :]
    joined = jnp.where(row_pos <= col_pos, pairs_now, pairs_past)
    doubled = jnp.concatenate([joined, joined], axis=2).reshape(group_count, 2 * taps * taps)
    padded = jnp.concatenate([doubled, jnp.zeros((group_count, taps), jnp.float32)], axis=1)
    skewed = padded.reshape(group_count, taps, 2 * taps + 1)[:, :, :taps]
    return jnp.sum(skewed, axis=1)


def short_mix(field, taps_row):
    tap_count = taps_row.shape[0]
    extra = tap_count - 1
    row_count = field.shape[1]
    padded = jnp.concatenate([jnp.zeros((field.shape[0], extra), field.dtype), field], axis=1)
    total = jnp.zeros(field.shape, jnp.float32)
    for tap_index in range(tap_count):
        start = extra - tap_index
        total = total + taps_row[tap_index].astype(jnp.float32)[:, None] * padded[
            :, start : start + row_count
        ].astype(jnp.float32)
    return total


def short_back(field, taps_row):
    tap_count = taps_row.shape[0]
    extra = tap_count - 1
    row_count = field.shape[1]
    padded = jnp.concatenate([field, jnp.zeros((field.shape[0], extra), field.dtype)], axis=1)
    total = jnp.zeros(field.shape, jnp.float32)
    for tap_index in range(tap_count):
        total = total + taps_row[tap_index].astype(jnp.float32)[:, None] * padded[
            :, tap_index : tap_index + row_count
        ].astype(jnp.float32)
    return total


def short_corr(grad, field, tap_count):
    extra = tap_count - 1
    row_count = field.shape[1]
    padded = jnp.concatenate([jnp.zeros((field.shape[0], extra), field.dtype), field], axis=1)
    grad_wide = grad.astype(jnp.float32)
    rows_out = []
    for tap_index in range(tap_count):
        start = extra - tap_index
        rows_out.append(
            jnp.sum(grad_wide * padded[:, start : start + row_count].astype(jnp.float32), axis=1)
        )
    return jnp.stack(rows_out)


CHUNKS = 2


def short_corr_rows(grad, field, tap_count):
    extra = tap_count - 1
    row_count = field.shape[0]
    padded = jnp.concatenate([jnp.zeros((extra, field.shape[1]), field.dtype), field], axis=0)
    grad_wide = grad.astype(jnp.float32)
    rows_out = []
    for tap_index in range(tap_count):
        start = extra - tap_index
        rows_out.append(
            jnp.sum(grad_wide * padded[start : start + row_count].astype(jnp.float32), axis=0)
        )
    return jnp.stack(rows_out)


def body(section_input, out_grad, short_filter, long_filter):
    devices = lax.axis_size("dp")
    rows, width = section_input.shape[1], section_input.shape[2]
    short_all = short_filter[0]
    long_all = long_filter[0]
    group_count, taps = (long_all.shape[1], long_all.shape[2])
    tap_count = short_all.shape[1]
    circ_now, circ_past = circulants(long_all)
    grad_rows = lax.all_to_all(out_grad[0], "dp", split_axis=1, concat_axis=0, tiled=True)
    grad_rows, later_input = lax.optimization_barrier((grad_rows, section_input[0]))
    input_rows = lax.all_to_all(later_input, "dp", split_axis=1, concat_axis=0, tiled=True)
    top_grad = grad_rows.T
    own = top_grad.shape[0]
    half = own // 2
    group_half = group_count // 2
    dmix_twos, middle_grads, dmix_ones, behinds = [], [], [], []
    for index in range(2):
        rows_of = slice(index * half, (index + 1) * half)
        groups_of = slice(index * group_half, (index + 1) * group_half)
        grad_half = top_grad[rows_of]
        if index:
            grad_half, input_grad_h = lax.optimization_barrier((grad_half, input_grad_h))
            behinds.append(from_behind(input_grad_h, "pipe", -1))
        short_half = short_all[:, :, rows_of]
        dmix_two_h = anti_long(grad_half, circ_now[1, groups_of], circ_past[1, groups_of]).astype(jnp.bfloat16)
        middle_grad_h = (
            grad_half.astype(jnp.float32) + short_back(dmix_two_h, short_half[1])
        ).astype(jnp.bfloat16)
        dmix_one_h = anti_long(middle_grad_h, circ_now[0, groups_of], circ_past[0, groups_of]).astype(
            jnp.bfloat16
        )
        input_grad_h = (
            middle_grad_h.astype(jnp.float32) + short_back(dmix_one_h, short_half[0])
        ).astype(jnp.bfloat16)
        dmix_twos.append(dmix_two_h)
        middle_grads.append(middle_grad_h)
        dmix_ones.append(dmix_one_h)
    dmix_two = jnp.concatenate(dmix_twos)
    middle_grad = jnp.concatenate(middle_grads)
    dmix_one = jnp.concatenate(dmix_ones)
    behinds.append(from_behind(input_grad_h, "pipe", -1))
    input_rows, _ = lax.optimization_barrier((input_rows, input_grad_h))
    source = input_rows.T
    mixed_one = short_mix(source, short_all[0]).astype(jnp.bfloat16)
    long_one = causal_long(mixed_one, circ_now[0], circ_past[0])
    middle = (source.astype(jnp.float32) + long_one).astype(jnp.bfloat16)
    mixed_two = short_mix(middle, short_all[1]).astype(jnp.bfloat16)
    behinds = list(lax.optimization_barrier((*behinds, mixed_two))[:-1])
    behind = jnp.concatenate(behinds)
    own_rows = lax.all_to_all(behind.T, "dp", split_axis=0, concat_axis=1, tiled=True)
    passed_grad = own_rows[None]
    dlong_two = lag_grad(mixed_two, top_grad, group_count, taps)
    dshort_two = short_corr_rows(dmix_two.T, middle.T, tap_count)
    dlong_one = lag_grad(mixed_one, middle_grad, group_count, taps)
    dshort_one = short_corr_rows(dmix_one.T, input_rows, tap_count)
    factor = float(rows * devices) ** (-0.5)
    short_grad = jnp.stack([dshort_one, dshort_two])[None] * factor
    long_grad = jnp.stack([dlong_one, dlong_two])[None] * factor
    return (passed_grad, short_grad, long_grad)


def solution(mesh):
    in_specs = (
        P("pipe", "dp", None),
        P("pipe", "dp", None),
        P("pipe", None, None, "dp"),
        P("pipe", None, "dp", None),
    )
    out_specs = (P("pipe", "dp", None), P("pipe", None, None, "dp"), P("pipe", None, "dp", None))
    return jax.shard_map(body, mesh=mesh, in_specs=in_specs, out_specs=out_specs, check_vma=False)
```

```python
import jax
import jax.numpy as jnp
from jax import lax
from jax.sharding import PartitionSpec as P


def from_behind(shard, axis, by):
    devices = lax.axis_size(axis)
    pairs = [(i, i + by) for i in range(devices) if 0 <= i + by < devices]
    return lax.ppermute(shard, axis, pairs)


def circulants(long_pair):
    pair_count, group_count, taps = long_pair.shape
    row_pos = jnp.arange(taps, dtype=jnp.int32)[:, None]
    col_pos = jnp.arange(taps, dtype=jnp.int32)[None, :]
    lag_table = (col_pos - row_pos + taps) % taps
    table = (lag_table.reshape(1, -1) == jnp.arange(taps, dtype=jnp.int32)[:, None]).astype(
        jnp.bfloat16
    )
    flat = jnp.dot(long_pair.reshape(-1, taps), table, preferred_element_type=jnp.float32).astype(
        jnp.bfloat16
    )
    circ = flat.reshape(pair_count, group_count, taps, taps)
    upper = row_pos <= col_pos
    zero_value = jnp.zeros((), jnp.bfloat16)
    return (jnp.where(upper, circ, zero_value), jnp.where(upper, zero_value, circ))


def as_groups(field, group_count, taps):
    return field.reshape(group_count, field.shape[0] // group_count, field.shape[1] // taps, taps)


def causal_long(field, circ_now, circ_past):
    group_count, taps = (circ_now.shape[0], circ_now.shape[2])
    blocks = as_groups(field, group_count, taps)
    earlier_blocks = jnp.concatenate([jnp.zeros_like(blocks[:, :, :1]), blocks[:, :, :-1]], axis=2)
    total = jnp.einsum("gcbt,gts->gcbs", blocks, circ_now, preferred_element_type=jnp.float32)
    total = total + jnp.einsum(
        "gcbt,gts->gcbs", earlier_blocks, circ_past, preferred_element_type=jnp.float32
    )
    return total.reshape(field.shape)


def anti_long(grad, circ_now, circ_past):
    group_count, taps = (circ_now.shape[0], circ_now.shape[2])
    blocks = as_groups(grad, group_count, taps)
    later_blocks = jnp.concatenate([blocks[:, :, 1:], jnp.zeros_like(blocks[:, :, :1])], axis=2)
    total = jnp.einsum("gcbs,gts->gcbt", blocks, circ_now, preferred_element_type=jnp.float32)
    total = total + jnp.einsum(
        "gcbs,gts->gcbt", later_blocks, circ_past, preferred_element_type=jnp.float32
    )
    return total.reshape(grad.shape)


def lag_grad(values, grad, group_count, taps):
    value_blocks = as_groups(values, group_count, taps)
    grad_blocks = as_groups(grad, group_count, taps)
    earlier_blocks = jnp.concatenate(
        [jnp.zeros_like(value_blocks[:, :, :1]), value_blocks[:, :, :-1]], axis=2
    )
    pairs_now = jnp.einsum(
        "gcbt,gcbs->gts", value_blocks, grad_blocks, preferred_element_type=jnp.float32
    )
    pairs_past = jnp.einsum(
        "gcbt,gcbs->gts", earlier_blocks, grad_blocks, preferred_element_type=jnp.float32
    )
    row_pos = jnp.arange(taps, dtype=jnp.int32)[:, None]
    col_pos = jnp.arange(taps, dtype=jnp.int32)[None, :]
    joined = jnp.where(row_pos <= col_pos, pairs_now, pairs_past)
    doubled = jnp.concatenate([joined, joined], axis=2).reshape(group_count, 2 * taps * taps)
    padded = jnp.concatenate([doubled, jnp.zeros((group_count, taps), jnp.float32)], axis=1)
    skewed = padded.reshape(group_count, taps, 2 * taps + 1)[:, :, :taps]
    return jnp.sum(skewed, axis=1)


def short_mix(field, taps_row):
    tap_count = taps_row.shape[0]
    extra = tap_count - 1
    row_count = field.shape[1]
    padded = jnp.concatenate([jnp.zeros((field.shape[0], extra), field.dtype), field], axis=1)
    total = jnp.zeros(field.shape, jnp.float32)
    for tap_index in range(tap_count):
        start = extra - tap_index
        total = total + taps_row[tap_index].astype(jnp.float32)[:, None] * padded[
            :, start : start + row_count
        ].astype(jnp.float32)
    return total


def short_back(field, taps_row):
    tap_count = taps_row.shape[0]
    extra = tap_count - 1
    row_count = field.shape[1]
    padded = jnp.concatenate([field, jnp.zeros((field.shape[0], extra), field.dtype)], axis=1)
    total = jnp.zeros(field.shape, jnp.float32)
    for tap_index in range(tap_count):
        total = total + taps_row[tap_index].astype(jnp.float32)[:, None] * padded[
            :, tap_index : tap_index + row_count
        ].astype(jnp.float32)
    return total


def short_corr(grad, field, tap_count):
    extra = tap_count - 1
    row_count = field.shape[1]
    padded = jnp.concatenate([jnp.zeros((field.shape[0], extra), field.dtype), field], axis=1)
    grad_wide = grad.astype(jnp.float32)
    rows_out = []
    for tap_index in range(tap_count):
        start = extra - tap_index
        rows_out.append(
            jnp.sum(grad_wide * padded[:, start : start + row_count].astype(jnp.float32), axis=1)
        )
    return jnp.stack(rows_out)


CHUNKS = 2


def short_corr_rows(grad, field, tap_count):
    extra = tap_count - 1
    row_count = field.shape[0]
    padded = jnp.concatenate([jnp.zeros((extra, field.shape[1]), field.dtype), field], axis=0)
    grad_wide = grad.astype(jnp.float32)
    rows_out = []
    for tap_index in range(tap_count):
        start = extra - tap_index
        rows_out.append(
            jnp.sum(grad_wide * padded[start : start + row_count].astype(jnp.float32), axis=0)
        )
    return jnp.stack(rows_out)


def body(section_input, out_grad, short_filter, long_filter):
    devices = lax.axis_size("dp")
    rows, width = section_input.shape[1], section_input.shape[2]
    short_all = short_filter[0]
    long_all = long_filter[0]
    group_count, taps = (long_all.shape[1], long_all.shape[2])
    tap_count = short_all.shape[1]
    circ_now, circ_past = circulants(long_all)
    grad_rows = lax.all_to_all(out_grad[0], "dp", split_axis=1, concat_axis=0, tiled=True)
    grad_rows, later_input = lax.optimization_barrier((grad_rows, section_input[0]))
    input_rows = lax.all_to_all(later_input, "dp", split_axis=1, concat_axis=0, tiled=True)
    top_grad = grad_rows.T
    own = top_grad.shape[0]
    half = own // 2
    group_half = group_count // 2
    dmix_twos, middle_grads, dmix_ones, behinds = [], [], [], []
    for index in range(2):
        rows_of = slice(index * half, (index + 1) * half)
        groups_of = slice(index * group_half, (index + 1) * group_half)
        grad_half = top_grad[rows_of]
        if index:
            grad_half, input_grad_h = lax.optimization_barrier((grad_half, input_grad_h))
            behinds.append(from_behind(input_grad_h, "pipe", -1))
        short_half = short_all[:, :, rows_of]
        dmix_two_h = anti_long(grad_half, circ_now[1, groups_of], circ_past[1, groups_of]).astype(jnp.bfloat16)
        middle_grad_h = (
            grad_half.astype(jnp.float32) + short_back(dmix_two_h, short_half[1])
        ).astype(jnp.bfloat16)
        dmix_one_h = anti_long(middle_grad_h, circ_now[0, groups_of], circ_past[0, groups_of]).astype(
            jnp.bfloat16
        )
        input_grad_h = (
            middle_grad_h.astype(jnp.float32) + short_back(dmix_one_h, short_half[0])
        ).astype(jnp.bfloat16)
        dmix_twos.append(dmix_two_h)
        middle_grads.append(middle_grad_h)
        dmix_ones.append(dmix_one_h)
    dmix_two = jnp.concatenate(dmix_twos)
    middle_grad = jnp.concatenate(middle_grads)
    dmix_one = jnp.concatenate(dmix_ones)
    behinds.append(from_behind(input_grad_h, "pipe", -1))
    input_rows, _, dmix_two_t, dmix_one_t, middle_grad = lax.optimization_barrier(
        (input_rows, input_grad_h, dmix_two.T, dmix_one.T, middle_grad)
    )
    behind = jnp.concatenate(behinds)
    own_rows = lax.all_to_all(behind.T, "dp", split_axis=0, concat_axis=1, tiled=True)
    passed_grad = own_rows[None]
    source = input_rows.T
    mixed_one = short_mix(source, short_all[0]).astype(jnp.bfloat16)
    long_one = causal_long(mixed_one, circ_now[0], circ_past[0])
    middle = (source.astype(jnp.float32) + long_one).astype(jnp.bfloat16)
    mixed_two = short_mix(middle, short_all[1]).astype(jnp.bfloat16)
    dlong_two = lag_grad(mixed_two, top_grad, group_count, taps)
    dshort_two = short_corr_rows(dmix_two_t, middle.T, tap_count)
    dlong_one = lag_grad(mixed_one, middle_grad, group_count, taps)
    dshort_one = short_corr_rows(dmix_one_t, input_rows, tap_count)
    factor = float(rows * devices) ** (-0.5)
    short_grad = jnp.stack([dshort_one, dshort_two])[None] * factor
    long_grad = jnp.stack([dlong_one, dlong_two])[None] * factor
    return (passed_grad, short_grad, long_grad)


def solution(mesh):
    in_specs = (
        P("pipe", "dp", None),
        P("pipe", "dp", None),
        P("pipe", None, None, "dp"),
        P("pipe", None, "dp", None),
    )
    out_specs = (P("pipe", "dp", None), P("pipe", None, None, "dp"), P("pipe", None, "dp", None))
    return jax.shard_map(body, mesh=mesh, in_specs=in_specs, out_specs=out_specs, check_vma=False)
```

```python
import jax
import jax.numpy as jnp
from jax import lax
from jax.sharding import PartitionSpec as P


def from_behind(shard, axis, by):
    devices = lax.axis_size(axis)
    pairs = [(i, i + by) for i in range(devices) if 0 <= i + by < devices]
    return lax.ppermute(shard, axis, pairs)


def circulants(long_pair):
    pair_count, group_count, taps = long_pair.shape
    row_pos = jnp.arange(taps, dtype=jnp.int32)[:, None]
    col_pos = jnp.arange(taps, dtype=jnp.int32)[None, :]
    lag_table = (col_pos - row_pos + taps) % taps
    table = (lag_table.reshape(1, -1) == jnp.arange(taps, dtype=jnp.int32)[:, None]).astype(
        jnp.bfloat16
    )
    flat = jnp.dot(long_pair.reshape(-1, taps), table, preferred_element_type=jnp.float32).astype(
        jnp.bfloat16
    )
    circ = flat.reshape(pair_count, group_count, taps, taps)
    upper = row_pos <= col_pos
    zero_value = jnp.zeros((), jnp.bfloat16)
    return (jnp.where(upper, circ, zero_value), jnp.where(upper, zero_value, circ))


def as_groups(field, group_count, taps):
    return field.reshape(group_count, field.shape[0] // group_count, field.shape[1] // taps, taps)


def causal_long(field, circ_now, circ_past):
    group_count, taps = (circ_now.shape[0], circ_now.shape[2])
    blocks = as_groups(field, group_count, taps)
    earlier_blocks = jnp.concatenate([jnp.zeros_like(blocks[:, :, :1]), blocks[:, :, :-1]], axis=2)
    total = jnp.einsum("gcbt,gts->gcbs", blocks, circ_now, preferred_element_type=jnp.float32)
    total = total + jnp.einsum(
        "gcbt,gts->gcbs", earlier_blocks, circ_past, preferred_element_type=jnp.float32
    )
    return total.reshape(field.shape)


def anti_long(grad, circ_now, circ_past):
    group_count, taps = (circ_now.shape[0], circ_now.shape[2])
    blocks = as_groups(grad, group_count, taps)
    later_blocks = jnp.concatenate([blocks[:, :, 1:], jnp.zeros_like(blocks[:, :, :1])], axis=2)
    total = jnp.einsum("gcbs,gts->gcbt", blocks, circ_now, preferred_element_type=jnp.float32)
    total = total + jnp.einsum(
        "gcbs,gts->gcbt", later_blocks, circ_past, preferred_element_type=jnp.float32
    )
    return total.reshape(grad.shape)


def lag_grad(values, grad, group_count, taps):
    value_blocks = as_groups(values, group_count, taps)
    grad_blocks = as_groups(grad, group_count, taps)
    earlier_blocks = jnp.concatenate(
        [jnp.zeros_like(value_blocks[:, :, :1]), value_blocks[:, :, :-1]], axis=2
    )
    pairs_now = jnp.einsum(
        "gcbt,gcbs->gts", value_blocks, grad_blocks, preferred_element_type=jnp.float32
    )
    pairs_past = jnp.einsum(
        "gcbt,gcbs->gts", earlier_blocks, grad_blocks, preferred_element_type=jnp.float32
    )
    row_pos = jnp.arange(taps, dtype=jnp.int32)[:, None]
    col_pos = jnp.arange(taps, dtype=jnp.int32)[None, :]
    joined = jnp.where(row_pos <= col_pos, pairs_now, pairs_past)
    doubled = jnp.concatenate([joined, joined], axis=2).reshape(group_count, 2 * taps * taps)
    padded = jnp.concatenate([doubled, jnp.zeros((group_count, taps), jnp.float32)], axis=1)
    skewed = padded.reshape(group_count, taps, 2 * taps + 1)[:, :, :taps]
    return jnp.sum(skewed, axis=1)


def short_mix(field, taps_row):
    tap_count = taps_row.shape[0]
    extra = tap_count - 1
    row_count = field.shape[1]
    padded = jnp.concatenate([jnp.zeros((field.shape[0], extra), field.dtype), field], axis=1)
    total = jnp.zeros(field.shape, jnp.float32)
    for tap_index in range(tap_count):
        start = extra - tap_index
        total = total + taps_row[tap_index].astype(jnp.float32)[:, None] * padded[
            :, start : start + row_count
        ].astype(jnp.float32)
    return total


def short_back(field, taps_row):
    tap_count = taps_row.shape[0]
    extra = tap_count - 1
    row_count = field.shape[1]
    padded = jnp.concatenate([field, jnp.zeros((field.shape[0], extra), field.dtype)], axis=1)
    total = jnp.zeros(field.shape, jnp.float32)
    for tap_index in range(tap_count):
        total = total + taps_row[tap_index].astype(jnp.float32)[:, None] * padded[
            :, tap_index : tap_index + row_count
        ].astype(jnp.float32)
    return total


def short_corr(grad, field, tap_count):
    extra = tap_count - 1
    row_count = field.shape[1]
    padded = jnp.concatenate([jnp.zeros((field.shape[0], extra), field.dtype), field], axis=1)
    grad_wide = grad.astype(jnp.float32)
    rows_out = []
    for tap_index in range(tap_count):
        start = extra - tap_index
        rows_out.append(
            jnp.sum(grad_wide * padded[:, start : start + row_count].astype(jnp.float32), axis=1)
        )
    return jnp.stack(rows_out)


CHUNKS = 2


def short_corr_rows(grad, field, tap_count):
    extra = tap_count - 1
    row_count = field.shape[0]
    padded = jnp.concatenate([jnp.zeros((extra, field.shape[1]), field.dtype), field], axis=0)
    grad_wide = grad.astype(jnp.float32)
    rows_out = []
    for tap_index in range(tap_count):
        start = extra - tap_index
        rows_out.append(
            jnp.sum(grad_wide * padded[start : start + row_count].astype(jnp.float32), axis=0)
        )
    return jnp.stack(rows_out)


def body(section_input, out_grad, short_filter, long_filter):
    devices = lax.axis_size("dp")
    rows, width = section_input.shape[1], section_input.shape[2]
    short_all = short_filter[0]
    long_all = long_filter[0]
    group_count, taps = (long_all.shape[1], long_all.shape[2])
    tap_count = short_all.shape[1]
    circ_now, circ_past = circulants(long_all)
    grad_rows = lax.all_to_all(out_grad[0], "dp", split_axis=1, concat_axis=0, tiled=True)
    grad_rows, later_input = lax.optimization_barrier((grad_rows, section_input[0]))
    input_rows = lax.all_to_all(later_input, "dp", split_axis=1, concat_axis=0, tiled=True)
    top_grad = grad_rows.T
    own = top_grad.shape[0]
    half = own // 2
    group_half = group_count // 2
    dmix_twos, middle_grads, dmix_ones, behinds = [], [], [], []
    for index in range(2):
        rows_of = slice(index * half, (index + 1) * half)
        groups_of = slice(index * group_half, (index + 1) * group_half)
        grad_half = top_grad[rows_of]
        if index:
            grad_half, input_grad_h = lax.optimization_barrier((grad_half, input_grad_h))
            behinds.append(from_behind(input_grad_h, "pipe", -1))
        short_half = short_all[:, :, rows_of]
        dmix_two_h = anti_long(grad_half, circ_now[1, groups_of], circ_past[1, groups_of]).astype(jnp.bfloat16)
        middle_grad_h = (
            grad_half.astype(jnp.float32) + short_back(dmix_two_h, short_half[1])
        ).astype(jnp.bfloat16)
        dmix_one_h = anti_long(middle_grad_h, circ_now[0, groups_of], circ_past[0, groups_of]).astype(
            jnp.bfloat16
        )
        input_grad_h = (
            middle_grad_h.astype(jnp.float32) + short_back(dmix_one_h, short_half[0])
        ).astype(jnp.bfloat16)
        dmix_twos.append(dmix_two_h)
        middle_grads.append(middle_grad_h)
        dmix_ones.append(dmix_one_h)
    dmix_two = jnp.concatenate(dmix_twos)
    middle_grad = jnp.concatenate(middle_grads)
    dmix_one = jnp.concatenate(dmix_ones)
    behinds.append(from_behind(input_grad_h, "pipe", -1))
    input_rows, _ = lax.optimization_barrier((input_rows, input_grad_h))
    source = input_rows.T
    mixed_one = short_mix(source, short_all[0]).astype(jnp.bfloat16)
    long_one = causal_long(mixed_one, circ_now[0], circ_past[0])
    middle = (source.astype(jnp.float32) + long_one).astype(jnp.bfloat16)
    mixed_two = short_mix(middle, short_all[1]).astype(jnp.bfloat16)
    behinds = list(lax.optimization_barrier((*behinds, middle))[:-1])
    behind = jnp.concatenate(behinds)
    own_rows = lax.all_to_all(behind.T, "dp", split_axis=0, concat_axis=1, tiled=True)
    passed_grad = own_rows[None]
    dlong_two = lag_grad(mixed_two, top_grad, group_count, taps)
    dshort_two = short_corr_rows(dmix_two.T, middle.T, tap_count)
    dlong_one = lag_grad(mixed_one, middle_grad, group_count, taps)
    dshort_one = short_corr_rows(dmix_one.T, input_rows, tap_count)
    factor = float(rows * devices) ** (-0.5)
    short_grad = jnp.stack([dshort_one, dshort_two])[None] * factor
    long_grad = jnp.stack([dlong_one, dlong_two])[None] * factor
    return (passed_grad, short_grad, long_grad)


def solution(mesh):
    in_specs = (
        P("pipe", "dp", None),
        P("pipe", "dp", None),
        P("pipe", None, None, "dp"),
        P("pipe", None, "dp", None),
    )
    out_specs = (P("pipe", "dp", None), P("pipe", None, None, "dp"), P("pipe", None, "dp", None))
    return jax.shard_map(body, mesh=mesh, in_specs=in_specs, out_specs=out_specs, check_vma=False)
```

```python
import jax
import jax.numpy as jnp
from jax import lax
from jax.sharding import PartitionSpec as P


def from_behind(shard, axis, by):
    devices = lax.axis_size(axis)
    pairs = [(i, i + by) for i in range(devices) if 0 <= i + by < devices]
    return lax.ppermute(shard, axis, pairs)


def circulants(long_pair):
    pair_count, group_count, taps = long_pair.shape
    row_pos = jnp.arange(taps, dtype=jnp.int32)[:, None]
    col_pos = jnp.arange(taps, dtype=jnp.int32)[None, :]
    lag_table = (col_pos - row_pos + taps) % taps
    table = (lag_table.reshape(1, -1) == jnp.arange(taps, dtype=jnp.int32)[:, None]).astype(
        jnp.bfloat16
    )
    flat = jnp.dot(long_pair.reshape(-1, taps), table, preferred_element_type=jnp.float32).astype(
        jnp.bfloat16
    )
    circ = flat.reshape(pair_count, group_count, taps, taps)
    upper = row_pos <= col_pos
    zero_value = jnp.zeros((), jnp.bfloat16)
    return (jnp.where(upper, circ, zero_value), jnp.where(upper, zero_value, circ))


def as_groups(field, group_count, taps):
    return field.reshape(group_count, field.shape[0] // group_count, field.shape[1] // taps, taps)


def causal_long(field, circ_now, circ_past):
    group_count, taps = (circ_now.shape[0], circ_now.shape[2])
    blocks = as_groups(field, group_count, taps)
    earlier_blocks = jnp.concatenate([jnp.zeros_like(blocks[:, :, :1]), blocks[:, :, :-1]], axis=2)
    total = jnp.einsum("gcbt,gts->gcbs", blocks, circ_now, preferred_element_type=jnp.float32)
    total = total + jnp.einsum(
        "gcbt,gts->gcbs", earlier_blocks, circ_past, preferred_element_type=jnp.float32
    )
    return total.reshape(field.shape)


def anti_long(grad, circ_now, circ_past):
    group_count, taps = (circ_now.shape[0], circ_now.shape[2])
    blocks = as_groups(grad, group_count, taps)
    later_blocks = jnp.concatenate([blocks[:, :, 1:], jnp.zeros_like(blocks[:, :, :1])], axis=2)
    total = jnp.einsum("gcbs,gts->gcbt", blocks, circ_now, preferred_element_type=jnp.float32)
    total = total + jnp.einsum(
        "gcbs,gts->gcbt", later_blocks, circ_past, preferred_element_type=jnp.float32
    )
    return total.reshape(grad.shape)


def lag_grad(values, grad, group_count, taps):
    value_blocks = as_groups(values, group_count, taps)
    grad_blocks = as_groups(grad, group_count, taps)
    earlier_blocks = jnp.concatenate(
        [jnp.zeros_like(value_blocks[:, :, :1]), value_blocks[:, :, :-1]], axis=2
    )
    pairs_now = jnp.einsum(
        "gcbt,gcbs->gts", value_blocks, grad_blocks, preferred_element_type=jnp.float32
    )
    pairs_past = jnp.einsum(
        "gcbt,gcbs->gts", earlier_blocks, grad_blocks, preferred_element_type=jnp.float32
    )
    row_pos = jnp.arange(taps, dtype=jnp.int32)[:, None]
    col_pos = jnp.arange(taps, dtype=jnp.int32)[None, :]
    joined = jnp.where(row_pos <= col_pos, pairs_now, pairs_past)
    doubled = jnp.concatenate([joined, joined], axis=2).reshape(group_count, 2 * taps * taps)
    padded = jnp.concatenate([doubled, jnp.zeros((group_count, taps), jnp.float32)], axis=1)
    skewed = padded.reshape(group_count, taps, 2 * taps + 1)[:, :, :taps]
    return jnp.sum(skewed, axis=1)


def short_mix(field, taps_row):
    tap_count = taps_row.shape[0]
    extra = tap_count - 1
    row_count = field.shape[1]
    padded = jnp.concatenate([jnp.zeros((field.shape[0], extra), field.dtype), field], axis=1)
    total = jnp.zeros(field.shape, jnp.float32)
    for tap_index in range(tap_count):
        start = extra - tap_index
        total = total + taps_row[tap_index].astype(jnp.float32)[:, None] * padded[
            :, start : start + row_count
        ].astype(jnp.float32)
    return total


def short_back(field, taps_row):
    tap_count = taps_row.shape[0]
    extra = tap_count - 1
    row_count = field.shape[1]
    padded = jnp.concatenate([field, jnp.zeros((field.shape[0], extra), field.dtype)], axis=1)
    total = jnp.zeros(field.shape, jnp.float32)
    for tap_index in range(tap_count):
        total = total + taps_row[tap_index].astype(jnp.float32)[:, None] * padded[
            :, tap_index : tap_index + row_count
        ].astype(jnp.float32)
    return total


def short_corr(grad, field, tap_count):
    extra = tap_count - 1
    row_count = field.shape[1]
    padded = jnp.concatenate([jnp.zeros((field.shape[0], extra), field.dtype), field], axis=1)
    grad_wide = grad.astype(jnp.float32)
    rows_out = []
    for tap_index in range(tap_count):
        start = extra - tap_index
        rows_out.append(
            jnp.sum(grad_wide * padded[:, start : start + row_count].astype(jnp.float32), axis=1)
        )
    return jnp.stack(rows_out)


CHUNKS = 2


def short_corr_rows(grad, field, tap_count):
    extra = tap_count - 1
    row_count = field.shape[0]
    padded = jnp.concatenate([jnp.zeros((extra, field.shape[1]), field.dtype), field], axis=0)
    grad_wide = grad.astype(jnp.float32)
    rows_out = []
    for tap_index in range(tap_count):
        start = extra - tap_index
        rows_out.append(
            jnp.sum(grad_wide * padded[start : start + row_count].astype(jnp.float32), axis=0)
        )
    return jnp.stack(rows_out)


def body(section_input, out_grad, short_filter, long_filter):
    devices = lax.axis_size("dp")
    rows, width = section_input.shape[1], section_input.shape[2]
    short_all = short_filter[0]
    long_all = long_filter[0]
    group_count, taps = (long_all.shape[1], long_all.shape[2])
    tap_count = short_all.shape[1]
    circ_now, circ_past = circulants(long_all)
    grad_rows = lax.all_to_all(out_grad[0], "dp", split_axis=1, concat_axis=0, tiled=True)
    grad_rows, later_input = lax.optimization_barrier((grad_rows, section_input[0]))
    input_rows = lax.all_to_all(later_input, "dp", split_axis=1, concat_axis=0, tiled=True)
    top_grad = grad_rows.T
    own = top_grad.shape[0]
    half = own // 2
    group_half = group_count // 2
    dmix_twos, middle_grads, dmix_ones, behinds = [], [], [], []
    for index in range(2):
        rows_of = slice(index * half, (index + 1) * half)
        groups_of = slice(index * group_half, (index + 1) * group_half)
        grad_half = top_grad[rows_of]
        if index:
            grad_half, input_grad_h = lax.optimization_barrier((grad_half, input_grad_h))
            behinds.append(from_behind(input_grad_h.T, "pipe", -1))
        short_half = short_all[:, :, rows_of]
        dmix_two_h = anti_long(grad_half, circ_now[1, groups_of], circ_past[1, groups_of]).astype(jnp.bfloat16)
        middle_grad_h = (
            grad_half.astype(jnp.float32) + short_back(dmix_two_h, short_half[1])
        ).astype(jnp.bfloat16)
        dmix_one_h = anti_long(middle_grad_h, circ_now[0, groups_of], circ_past[0, groups_of]).astype(
            jnp.bfloat16
        )
        input_grad_h = (
            middle_grad_h.astype(jnp.float32) + short_back(dmix_one_h, short_half[0])
        ).astype(jnp.bfloat16)
        dmix_twos.append(dmix_two_h)
        middle_grads.append(middle_grad_h)
        dmix_ones.append(dmix_one_h)
    dmix_two = jnp.concatenate(dmix_twos)
    middle_grad = jnp.concatenate(middle_grads)
    dmix_one = jnp.concatenate(dmix_ones)
    behinds.append(from_behind(input_grad_h.T, "pipe", -1))
    input_rows, _ = lax.optimization_barrier((input_rows, input_grad_h))
    source = input_rows.T
    mixed_one = short_mix(source, short_all[0]).astype(jnp.bfloat16)
    long_one = causal_long(mixed_one, circ_now[0], circ_past[0])
    middle = (source.astype(jnp.float32) + long_one).astype(jnp.bfloat16)
    mixed_two = short_mix(middle, short_all[1]).astype(jnp.bfloat16)
    behinds = list(lax.optimization_barrier((*behinds, middle))[:-1])
    behind = jnp.concatenate(behinds, axis=1)
    own_rows = lax.all_to_all(behind, "dp", split_axis=0, concat_axis=1, tiled=True)
    passed_grad = own_rows[None]
    dlong_two = lag_grad(mixed_two, top_grad, group_count, taps)
    dshort_two = short_corr_rows(dmix_two.T, middle.T, tap_count)
    dlong_one = lag_grad(mixed_one, middle_grad, group_count, taps)
    dshort_one = short_corr_rows(dmix_one.T, input_rows, tap_count)
    factor = float(rows * devices) ** (-0.5)
    short_grad = jnp.stack([dshort_one, dshort_two])[None] * factor
    long_grad = jnp.stack([dlong_one, dlong_two])[None] * factor
    return (passed_grad, short_grad, long_grad)


def solution(mesh):
    in_specs = (
        P("pipe", "dp", None),
        P("pipe", "dp", None),
        P("pipe", None, None, "dp"),
        P("pipe", None, "dp", None),
    )
    out_specs = (P("pipe", "dp", None), P("pipe", None, None, "dp"), P("pipe", None, "dp", None))
    return jax.shard_map(body, mesh=mesh, in_specs=in_specs, out_specs=out_specs, check_vma=False)
```

```python
import jax
import jax.numpy as jnp
from jax import lax
from jax.sharding import PartitionSpec as P


def from_behind(shard, axis, by):
    devices = lax.axis_size(axis)
    pairs = [(i, i + by) for i in range(devices) if 0 <= i + by < devices]
    return lax.ppermute(shard, axis, pairs)


def circulants(long_pair):
    pair_count, group_count, taps = long_pair.shape
    row_pos = jnp.arange(taps, dtype=jnp.int32)[:, None]
    col_pos = jnp.arange(taps, dtype=jnp.int32)[None, :]
    lag_table = (col_pos - row_pos + taps) % taps
    table = (lag_table.reshape(1, -1) == jnp.arange(taps, dtype=jnp.int32)[:, None]).astype(
        jnp.bfloat16
    )
    flat = jnp.dot(long_pair.reshape(-1, taps), table, preferred_element_type=jnp.float32).astype(
        jnp.bfloat16
    )
    circ = flat.reshape(pair_count, group_count, taps, taps)
    upper = row_pos <= col_pos
    zero_value = jnp.zeros((), jnp.bfloat16)
    return (jnp.where(upper, circ, zero_value), jnp.where(upper, zero_value, circ))


def as_groups(field, group_count, taps):
    return field.reshape(group_count, field.shape[0] // group_count, field.shape[1] // taps, taps)


def causal_long(field, circ_now, circ_past):
    group_count, taps = (circ_now.shape[0], circ_now.shape[2])
    blocks = as_groups(field, group_count, taps)
    earlier_blocks = jnp.concatenate([jnp.zeros_like(blocks[:, :, :1]), blocks[:, :, :-1]], axis=2)
    total = jnp.einsum("gcbt,gts->gcbs", blocks, circ_now, preferred_element_type=jnp.float32)
    total = total + jnp.einsum(
        "gcbt,gts->gcbs", earlier_blocks, circ_past, preferred_element_type=jnp.float32
    )
    return total.reshape(field.shape)


def anti_long(grad, circ_now, circ_past):
    group_count, taps = (circ_now.shape[0], circ_now.shape[2])
    blocks = as_groups(grad, group_count, taps)
    later_blocks = jnp.concatenate([blocks[:, :, 1:], jnp.zeros_like(blocks[:, :, :1])], axis=2)
    total = jnp.einsum("gcbs,gts->gcbt", blocks, circ_now, preferred_element_type=jnp.float32)
    total = total + jnp.einsum(
        "gcbs,gts->gcbt", later_blocks, circ_past, preferred_element_type=jnp.float32
    )
    return total.reshape(grad.shape)


def lag_grad(values, grad, group_count, taps):
    value_blocks = as_groups(values, group_count, taps)
    grad_blocks = as_groups(grad, group_count, taps)
    earlier_blocks = jnp.concatenate(
        [jnp.zeros_like(value_blocks[:, :, :1]), value_blocks[:, :, :-1]], axis=2
    )
    pairs_now = jnp.einsum(
        "gcbt,gcbs->gts", value_blocks, grad_blocks, preferred_element_type=jnp.float32
    )
    pairs_past = jnp.einsum(
        "gcbt,gcbs->gts", earlier_blocks, grad_blocks, preferred_element_type=jnp.float32
    )
    row_pos = jnp.arange(taps, dtype=jnp.int32)[:, None]
    col_pos = jnp.arange(taps, dtype=jnp.int32)[None, :]
    joined = jnp.where(row_pos <= col_pos, pairs_now, pairs_past)
    doubled = jnp.concatenate([joined, joined], axis=2).reshape(group_count, 2 * taps * taps)
    padded = jnp.concatenate([doubled, jnp.zeros((group_count, taps), jnp.float32)], axis=1)
    skewed = padded.reshape(group_count, taps, 2 * taps + 1)[:, :, :taps]
    return jnp.sum(skewed, axis=1)


def short_mix(field, taps_row):
    tap_count = taps_row.shape[0]
    extra = tap_count - 1
    row_count = field.shape[1]
    padded = jnp.concatenate([jnp.zeros((field.shape[0], extra), field.dtype), field], axis=1)
    total = jnp.zeros(field.shape, jnp.float32)
    for tap_index in range(tap_count):
        start = extra - tap_index
        total = total + taps_row[tap_index].astype(jnp.float32)[:, None] * padded[
            :, start : start + row_count
        ].astype(jnp.float32)
    return total


def short_back(field, taps_row):
    tap_count = taps_row.shape[0]
    extra = tap_count - 1
    row_count = field.shape[1]
    padded = jnp.concatenate([field, jnp.zeros((field.shape[0], extra), field.dtype)], axis=1)
    total = jnp.zeros(field.shape, jnp.float32)
    for tap_index in range(tap_count):
        total = total + taps_row[tap_index].astype(jnp.float32)[:, None] * padded[
            :, tap_index : tap_index + row_count
        ].astype(jnp.float32)
    return total


def short_corr(grad, field, tap_count):
    extra = tap_count - 1
    row_count = field.shape[1]
    padded = jnp.concatenate([jnp.zeros((field.shape[0], extra), field.dtype), field], axis=1)
    grad_wide = grad.astype(jnp.float32)
    rows_out = []
    for tap_index in range(tap_count):
        start = extra - tap_index
        rows_out.append(
            jnp.sum(grad_wide * padded[:, start : start + row_count].astype(jnp.float32), axis=1)
        )
    return jnp.stack(rows_out)


CHUNKS = 2


def short_corr_rows(grad, field, tap_count):
    extra = tap_count - 1
    row_count = field.shape[0]
    padded = jnp.concatenate([jnp.zeros((extra, field.shape[1]), field.dtype), field], axis=0)
    grad_wide = grad.astype(jnp.float32)
    rows_out = []
    for tap_index in range(tap_count):
        start = extra - tap_index
        rows_out.append(
            jnp.sum(grad_wide * padded[start : start + row_count].astype(jnp.float32), axis=0)
        )
    return jnp.stack(rows_out)


def body(section_input, out_grad, short_filter, long_filter):
    devices = lax.axis_size("dp")
    rows, width = section_input.shape[1], section_input.shape[2]
    short_all = short_filter[0]
    long_all = long_filter[0]
    group_count, taps = (long_all.shape[1], long_all.shape[2])
    tap_count = short_all.shape[1]
    circ_now, circ_past = circulants(long_all)
    grad_rows = lax.all_to_all(out_grad[0], "dp", split_axis=1, concat_axis=0, tiled=True)
    grad_rows, later_input = lax.optimization_barrier((grad_rows, section_input[0]))
    input_rows = lax.all_to_all(later_input, "dp", split_axis=1, concat_axis=0, tiled=True)
    top_grad = grad_rows.T
    own = top_grad.shape[0]
    half = own // 2
    group_half = group_count // 2
    dmix_twos, middle_grads, dmix_ones, behinds = [], [], [], []
    for index in range(2):
        rows_of = slice(index * half, (index + 1) * half)
        groups_of = slice(index * group_half, (index + 1) * group_half)
        grad_half = top_grad[rows_of]
        if index:
            grad_half, input_grad_h = lax.optimization_barrier((grad_half, input_grad_h))
            behinds.append(from_behind(input_grad_h, "pipe", -1))
        short_half = short_all[:, :, rows_of]
        dmix_two_h = anti_long(grad_half, circ_now[1, groups_of], circ_past[1, groups_of]).astype(jnp.bfloat16)
        middle_grad_h = (
            grad_half.astype(jnp.float32) + short_back(dmix_two_h, short_half[1])
        ).astype(jnp.bfloat16)
        dmix_one_h = anti_long(middle_grad_h, circ_now[0, groups_of], circ_past[0, groups_of]).astype(
            jnp.bfloat16
        )
        input_grad_h = (
            middle_grad_h.astype(jnp.float32) + short_back(dmix_one_h, short_half[0])
        ).astype(jnp.bfloat16)
        dmix_twos.append(dmix_two_h)
        middle_grads.append(middle_grad_h)
        dmix_ones.append(dmix_one_h)
    dmix_two = jnp.concatenate(dmix_twos)
    middle_grad = jnp.concatenate(middle_grads)
    dmix_one = jnp.concatenate(dmix_ones)
    behinds.append(from_behind(input_grad_h, "pipe", -1))
    input_rows, _ = lax.optimization_barrier((input_rows, input_grad_h))
    source = input_rows.T
    mixed_one = short_mix(source, short_all[0]).astype(jnp.bfloat16)
    long_one = causal_long(mixed_one, circ_now[0], circ_past[0])
    middle = (source.astype(jnp.float32) + long_one).astype(jnp.bfloat16)
    mixed_two = short_mix(middle, short_all[1]).astype(jnp.bfloat16)
    behinds = list(lax.optimization_barrier((*behinds, middle))[:-1])
    behind, dmix_two_t, dmix_one_t = lax.optimization_barrier(
        (jnp.concatenate(behinds), dmix_two.T, dmix_one.T)
    )
    own_rows = lax.all_to_all(behind.T, "dp", split_axis=0, concat_axis=1, tiled=True)
    passed_grad = own_rows[None]
    dlong_two = lag_grad(mixed_two, top_grad, group_count, taps)
    dshort_two = short_corr_rows(dmix_two_t, middle.T, tap_count)
    dlong_one = lag_grad(mixed_one, middle_grad, group_count, taps)
    dshort_one = short_corr_rows(dmix_one_t, input_rows, tap_count)
    factor = float(rows * devices) ** (-0.5)
    short_grad = jnp.stack([dshort_one, dshort_two])[None] * factor
    long_grad = jnp.stack([dlong_one, dlong_two])[None] * factor
    return (passed_grad, short_grad, long_grad)


def solution(mesh):
    in_specs = (
        P("pipe", "dp", None),
        P("pipe", "dp", None),
        P("pipe", None, None, "dp"),
        P("pipe", None, "dp", None),
    )
    out_specs = (P("pipe", "dp", None), P("pipe", None, None, "dp"), P("pipe", None, "dp", None))
    return jax.shard_map(body, mesh=mesh, in_specs=in_specs, out_specs=out_specs, check_vma=False)
```

```python
import jax
import jax.numpy as jnp
from jax import lax
from jax.sharding import PartitionSpec as P


def from_behind(shard, axis, by):
    devices = lax.axis_size(axis)
    pairs = [(i, i + by) for i in range(devices) if 0 <= i + by < devices]
    return lax.ppermute(shard, axis, pairs)


def circulants(long_pair):
    pair_count, group_count, taps = long_pair.shape
    row_pos = jnp.arange(taps, dtype=jnp.int32)[:, None]
    col_pos = jnp.arange(taps, dtype=jnp.int32)[None, :]
    lag_table = (col_pos - row_pos + taps) % taps
    table = (lag_table.reshape(1, -1) == jnp.arange(taps, dtype=jnp.int32)[:, None]).astype(
        jnp.bfloat16
    )
    flat = jnp.dot(long_pair.reshape(-1, taps), table, preferred_element_type=jnp.float32).astype(
        jnp.bfloat16
    )
    circ = flat.reshape(pair_count, group_count, taps, taps)
    upper = row_pos <= col_pos
    zero_value = jnp.zeros((), jnp.bfloat16)
    return (jnp.where(upper, circ, zero_value), jnp.where(upper, zero_value, circ))


def as_groups(field, group_count, taps):
    return field.reshape(group_count, field.shape[0] // group_count, field.shape[1] // taps, taps)


def causal_long(field, circ_now, circ_past):
    group_count, taps = (circ_now.shape[0], circ_now.shape[2])
    blocks = as_groups(field, group_count, taps)
    earlier_blocks = jnp.concatenate([jnp.zeros_like(blocks[:, :, :1]), blocks[:, :, :-1]], axis=2)
    total = jnp.einsum("gcbt,gts->gcbs", blocks, circ_now, preferred_element_type=jnp.float32)
    total = total + jnp.einsum(
        "gcbt,gts->gcbs", earlier_blocks, circ_past, preferred_element_type=jnp.float32
    )
    return total.reshape(field.shape)


def anti_long(grad, circ_now, circ_past):
    group_count, taps = (circ_now.shape[0], circ_now.shape[2])
    blocks = as_groups(grad, group_count, taps)
    later_blocks = jnp.concatenate([blocks[:, :, 1:], jnp.zeros_like(blocks[:, :, :1])], axis=2)
    total = jnp.einsum("gcbs,gts->gcbt", blocks, circ_now, preferred_element_type=jnp.float32)
    total = total + jnp.einsum(
        "gcbs,gts->gcbt", later_blocks, circ_past, preferred_element_type=jnp.float32
    )
    return total.reshape(grad.shape)


def lag_grad(values, grad, group_count, taps):
    value_blocks = as_groups(values, group_count, taps)
    grad_blocks = as_groups(grad, group_count, taps)
    earlier_blocks = jnp.concatenate(
        [jnp.zeros_like(value_blocks[:, :, :1]), value_blocks[:, :, :-1]], axis=2
    )
    pairs_now = jnp.einsum(
        "gcbt,gcbs->gts", value_blocks, grad_blocks, preferred_element_type=jnp.float32
    )
    pairs_past = jnp.einsum(
        "gcbt,gcbs->gts", earlier_blocks, grad_blocks, preferred_element_type=jnp.float32
    )
    row_pos = jnp.arange(taps, dtype=jnp.int32)[:, None]
    col_pos = jnp.arange(taps, dtype=jnp.int32)[None, :]
    joined = jnp.where(row_pos <= col_pos, pairs_now, pairs_past)
    doubled = jnp.concatenate([joined, joined], axis=2).reshape(group_count, 2 * taps * taps)
    padded = jnp.concatenate([doubled, jnp.zeros((group_count, taps), jnp.float32)], axis=1)
    skewed = padded.reshape(group_count, taps, 2 * taps + 1)[:, :, :taps]
    return jnp.sum(skewed, axis=1)


def short_mix(field, taps_row):
    tap_count = taps_row.shape[0]
    extra = tap_count - 1
    row_count = field.shape[1]
    padded = jnp.concatenate([jnp.zeros((field.shape[0], extra), field.dtype), field], axis=1)
    total = jnp.zeros(field.shape, jnp.float32)
    for tap_index in range(tap_count):
        start = extra - tap_index
        total = total + taps_row[tap_index].astype(jnp.float32)[:, None] * padded[
            :, start : start + row_count
        ].astype(jnp.float32)
    return total


def short_back(field, taps_row):
    tap_count = taps_row.shape[0]
    extra = tap_count - 1
    row_count = field.shape[1]
    padded = jnp.concatenate([field, jnp.zeros((field.shape[0], extra), field.dtype)], axis=1)
    total = jnp.zeros(field.shape, jnp.float32)
    for tap_index in range(tap_count):
        total = total + taps_row[tap_index].astype(jnp.float32)[:, None] * padded[
            :, tap_index : tap_index + row_count
        ].astype(jnp.float32)
    return total


def short_corr(grad, field, tap_count):
    extra = tap_count - 1
    row_count = field.shape[1]
    padded = jnp.concatenate([jnp.zeros((field.shape[0], extra), field.dtype), field], axis=1)
    grad_wide = grad.astype(jnp.float32)
    rows_out = []
    for tap_index in range(tap_count):
        start = extra - tap_index
        rows_out.append(
            jnp.sum(grad_wide * padded[:, start : start + row_count].astype(jnp.float32), axis=1)
        )
    return jnp.stack(rows_out)


CHUNKS = 2


def short_corr_rows(grad, field, tap_count):
    extra = tap_count - 1
    row_count = field.shape[0]
    padded = jnp.concatenate([jnp.zeros((extra, field.shape[1]), field.dtype), field], axis=0)
    grad_wide = grad.astype(jnp.float32)
    rows_out = []
    for tap_index in range(tap_count):
        start = extra - tap_index
        rows_out.append(
            jnp.sum(grad_wide * padded[start : start + row_count].astype(jnp.float32), axis=0)
        )
    return jnp.stack(rows_out)


def body(section_input, out_grad, short_filter, long_filter):
    devices = lax.axis_size("dp")
    rows, width = section_input.shape[1], section_input.shape[2]
    short_all = short_filter[0]
    long_all = long_filter[0]
    group_count, taps = (long_all.shape[1], long_all.shape[2])
    tap_count = short_all.shape[1]
    circ_now, circ_past = circulants(long_all)
    grad_rows = lax.all_to_all(out_grad[0], "dp", split_axis=1, concat_axis=0, tiled=True)
    grad_rows, later_input = lax.optimization_barrier((grad_rows, section_input[0]))
    input_rows = lax.all_to_all(later_input, "dp", split_axis=1, concat_axis=0, tiled=True)
    top_grad = grad_rows.T
    own = top_grad.shape[0]
    half = own // 2
    group_half = group_count // 2
    dmix_twos, middle_grads, dmix_ones, behinds = [], [], [], []
    for index in range(2):
        rows_of = slice(index * half, (index + 1) * half)
        groups_of = slice(index * group_half, (index + 1) * group_half)
        grad_half = top_grad[rows_of]
        if index:
            grad_half, input_grad_h = lax.optimization_barrier((grad_half, input_grad_h))
            behinds.append(from_behind(input_grad_h, "pipe", -1))
        short_half = short_all[:, :, rows_of]
        dmix_two_h = anti_long(grad_half, circ_now[1, groups_of], circ_past[1, groups_of]).astype(jnp.bfloat16)
        middle_grad_h = (
            grad_half.astype(jnp.float32) + short_back(dmix_two_h, short_half[1])
        ).astype(jnp.bfloat16)
        dmix_one_h = anti_long(middle_grad_h, circ_now[0, groups_of], circ_past[0, groups_of]).astype(
            jnp.bfloat16
        )
        input_grad_h = (
            middle_grad_h.astype(jnp.float32) + short_back(dmix_one_h, short_half[0])
        ).astype(jnp.bfloat16)
        dmix_twos.append(dmix_two_h)
        middle_grads.append(middle_grad_h)
        dmix_ones.append(dmix_one_h)
    dmix_two = jnp.concatenate(dmix_twos)
    middle_grad = jnp.concatenate(middle_grads)
    dmix_one = jnp.concatenate(dmix_ones)
    behinds.append(from_behind(input_grad_h, "pipe", -1))
    input_rows, _ = lax.optimization_barrier((input_rows, input_grad_h))
    source = input_rows.T
    mixed_one = short_mix(source, short_all[0]).astype(jnp.bfloat16)
    long_one = causal_long(mixed_one, circ_now[0], circ_past[0])
    middle = (source.astype(jnp.float32) + long_one).astype(jnp.bfloat16)
    mixed_two = short_mix(middle, short_all[1]).astype(jnp.bfloat16)
    behinds = list(lax.optimization_barrier((*behinds, mixed_one))[:-1])
    behind = jnp.concatenate(behinds)
    own_rows = lax.all_to_all(behind.T, "dp", split_axis=0, concat_axis=1, tiled=True)
    passed_grad = own_rows[None]
    dlong_two = lag_grad(mixed_two, top_grad, group_count, taps)
    dshort_two = short_corr_rows(dmix_two.T, middle.T, tap_count)
    dlong_one = lag_grad(mixed_one, middle_grad, group_count, taps)
    dshort_one = short_corr_rows(dmix_one.T, input_rows, tap_count)
    factor = float(rows * devices) ** (-0.5)
    short_grad = jnp.stack([dshort_one, dshort_two])[None] * factor
    long_grad = jnp.stack([dlong_one, dlong_two])[None] * factor
    return (passed_grad, short_grad, long_grad)


def solution(mesh):
    in_specs = (
        P("pipe", "dp", None),
        P("pipe", "dp", None),
        P("pipe", None, None, "dp"),
        P("pipe", None, "dp", None),
    )
    out_specs = (P("pipe", "dp", None), P("pipe", None, None, "dp"), P("pipe", None, "dp", None))
    return jax.shard_map(body, mesh=mesh, in_specs=in_specs, out_specs=out_specs, check_vma=False)
```
